512 devices in a mesh: pool: 128 (over x, z, core), tp: 4 (over y).
Axes of the slice: x: 4, y: 4, z: 16, core: 2. Of those that a mesh axis runs over, the one named last changes fastest.
Arguments:
- hidden_rows: bfloat16 [16384, 8192], P('pool', 'tp'), may hold values from -6 to 6
- kv_weight: bfloat16 [8192, 1024], P('tp', 'pool'), may hold values from -0.0625 to 0.0625
- queries: bfloat16 [16384, 4096], P('pool', 'tp'), may hold values from -5 to 5
- cache_table: bfloat16 [1024, 128, 1024], P('pool', None, 'tp'), may hold values from -5 to 5
- retrieval: int32 [128, 64], P('pool'), may hold values from 0 to 1023, as said below
- pattern: int32 [128, 2, 64], P('pool'), may hold values 0 or 1
Outputs:
- attended: bfloat16 [16384, 4096], P('pool', 'tp')
- fresh_kv: bfloat16 [16384, 1024], P('pool', 'tp')
The draws below stay inside these ranges and needn't reach their ends.
Inputs may be any that keep to these rules, and one draw needn't show every extreme that they name: `retrieval`: each request names 64 blocks held by 64 different devices (block b is held by device b // 8); one device, drawn from the seed, holds a block named by every request.
All inputs are finite; a program needn't handle non-finite values. No bound on the sum of `pattern` on one device may be relied on, other than what follows from the above.
Results may differ from the reference program's by a relative error of at most 0.025.
Values may be sent and summed in bfloat16 or wider, within the bound.
No kernel may reach another device: no remote copies, remote signals or barrier semaphores. Data moves between devices by JAX's collectives and lax.ppermute only.
A program may use at most 192 MiB of HBM per device.

```python
import jax
import jax.numpy as jnp
from jax import lax

D = 8192
HD = 128
QH = 32
KVH = 4
BLK = 128
RBLK = 64
R_BLOCKS = 2
CACHE_DEV = 8
R_DEV = 128
TOKENS = 16384
FETCH = 64
KVW = 1024
BLOCKS = 1024
N_POOL = 128


def draw_queries(key, part):
    shape = (TOKENS, QH * HD)
    first = jax.random.fold_in(key, 5)
    return jnp.clip(jax.random.normal(first, shape, jnp.float32), -5.0, 5.0).astype(jnp.bfloat16)


def draw_cache_table(key, part):
    shape = (BLOCKS, BLK, KVW)
    first = jax.random.fold_in(key, 3)
    return jnp.clip(jax.random.normal(first, shape, jnp.float32), -5.0, 5.0).astype(jnp.bfloat16)


def draw_retrieval(key, part):
    keys = jax.random.split(jax.random.fold_in(key, 11), 4)
    hot = jax.random.randint(keys[0], (), 0, N_POOL)
    columns = jnp.arange(N_POOL)[None, :]
    rows = jnp.arange(N_POOL)[:, None]
    raw = jax.random.randint(keys[1], (N_POOL, N_POOL), 0, 2 ** 20) * N_POOL + columns
    raw = jnp.where(columns == hot, -1, raw)
    raw = jnp.where((rows == 0) & (columns == 0), -2, raw)
    raw = jnp.where((rows == 1) & (columns == N_POOL - 1), -2, raw)
    owners = jnp.argsort(raw, axis=1)[:, :FETCH]
    mixing = jax.random.randint(keys[2], (N_POOL, FETCH), 0, 2 ** 20) * FETCH + jnp.arange(FETCH)[None, :]
    order = jnp.argsort(mixing, axis=1)
    owners = jnp.take_along_axis(owners, order, axis=1)
    local = jax.random.randint(keys[3], (N_POOL, FETCH), 0, CACHE_DEV)
    row_ids = jnp.arange(N_POOL)[:, None]
    local = jnp.where((row_ids == 0) & (owners == 0), 0, local)
    local = jnp.where((row_ids == 1) & (owners == N_POOL - 1), CACHE_DEV - 1, local)
    return (owners * CACHE_DEV + local).astype(jnp.int32)


def set_ends(drawn, rng, low, top_value):
    spot = [jax.random.randint(jax.random.fold_in(rng, axis), (), 0, length) for axis, length in enumerate(drawn.shape)]
    longest = drawn.shape.index(max(drawn.shape))
    neighbour = spot[:longest] + [(spot[longest] + 1) % drawn.shape[longest]] + spot[longest + 1:]
    return drawn.at[tuple(spot)].set(low).at[tuple(neighbour)].set(top_value)


def block_levels(stream_key, extent, cuts, low, top_value):
    def one(axis_at, blocks):
        draws = jax.random.uniform(jax.random.fold_in(jax.random.fold_in(stream_key, 6), axis_at), (blocks,), jnp.float32, low / len(cuts), top_value / len(cuts))
        return jnp.repeat(jnp.exp(draws), extent[axis_at] // blocks).reshape((-1,) + (1,) * (len(extent) - axis_at - 1))

    gain = one(*cuts[0])
    for cut in cuts[1:]:
        gain = gain * one(*cut)
    return gain


def normal_values(own_key, shape, scale, limit, pieces=(), kind=jnp.bfloat16):
    array = scale * jax.random.normal(own_key, shape, jnp.float32)
    if pieces:
        array = array * block_levels(own_key, shape, pieces, -0.22, 0.18)
    return jnp.clip(array, -limit, limit).astype(kind)


def setup_inputs(seed: int = 0) -> dict:
    arg_keys = jax.random.split(jax.random.key(seed), 7)
    hidden_rows = normal_values(arg_keys[0], (TOKENS, D), 1.0, 6.0, ((0, 128), (1, 4)))
    kv_weight = normal_values(arg_keys[1], (D, KVW), D ** -0.5, 0.0625, ((0, 4), (1, 128)))
    queries = draw_queries(jax.random.fold_in(arg_keys[6], 71), 0)
    cache_table = draw_cache_table(jax.random.fold_in(arg_keys[6], 71), 0)
    retrieval = draw_retrieval(jax.random.fold_in(arg_keys[6], 71), 0)
    pattern = set_ends((jax.random.randint(arg_keys[5], (N_POOL, R_BLOCKS, FETCH), 0, 2) < 1).astype(jnp.int32), jax.random.fold_in(arg_keys[5], 1), 0, 1)
    return {"hidden_rows": hidden_rows, "kv_weight": kv_weight, "queries": queries, "cache_table": cache_table, "retrieval": retrieval, "pattern": pattern}


def attend_request(q_rows, own_kv, fetched, pat):
    group = QH // KVH
    scale = float(HD) ** -0.5
    count = q_rows.shape[0]
    qh = q_rows.reshape(count, KVH, group, HD).astype(jnp.float32)
    far = fetched.reshape(FETCH * BLK, KVH, 2, HD)
    near = own_kv.reshape(count, KVH, 2, HD)
    keys = jnp.concatenate([far[:, :, 0], near[:, :, 0]], axis=0).astype(jnp.float32)
    vals = jnp.concatenate([far[:, :, 1], near[:, :, 1]], axis=0).astype(jnp.float32)
    scores = jnp.einsum("rhgd,shd->hgrs", qh, keys) * scale
    far_mask = jnp.repeat(jnp.repeat(pat != 0, RBLK, axis=0), BLK, axis=1)
    near_mask = jnp.arange(count)[:, None] >= jnp.arange(count)[None, :]
    mask = jnp.concatenate([far_mask, near_mask], axis=1)
    scores = jnp.where(mask[None, None], scores, -jnp.inf)
    top = jnp.max(scores, axis=-1, keepdims=True)
    weights = jnp.where(mask[None, None], jnp.exp(scores - top), 0.0)
    denom = jnp.sum(weights, axis=-1)
    rounded = weights.astype(jnp.bfloat16)
    rounded = lax.optimization_barrier(rounded).astype(jnp.float32)
    numer = jnp.einsum("hgrs,shd->rhgd", rounded, vals)
    result = numer / jnp.transpose(denom, (2, 0, 1))[:, :, :, None]
    return result.reshape(count, QH * HD).astype(jnp.bfloat16)


def reference(hidden_rows, kv_weight, queries, cache_table, retrieval, pattern):
    fresh_kv = jnp.dot(hidden_rows, kv_weight, preferred_element_type=jnp.float32).astype(jnp.bfloat16)

    def one_request(items):
        q_rows, own_kv, wanted, pat = items
        fetched = jnp.take(cache_table, wanted, axis=0)
        return attend_request(q_rows, own_kv, fetched, pat)

    attended = lax.map(one_request, (queries.reshape(N_POOL, R_DEV, QH * HD), fresh_kv.reshape(N_POOL, R_DEV, KVW), retrieval, pattern))
    return attended.reshape(TOKENS, QH * HD), fresh_kv
```

```python
import math

import jax
import jax.numpy as jnp
from jax import lax
from jax.sharding import PartitionSpec as P

HD = 128
QH = 32
KVH = 4
BLK = 128
RBLK = 64


def rows_by_keys(left, right):
    return lax.dot_general(
        left, right, (((1,), (1,)), ((), ())), preferred_element_type=jnp.float32
    )


def body(hidden_rows, kv_weight, queries, cache_table, retrieval, pattern):
    partial_kv = jnp.dot(
        hidden_rows,
        lax.all_gather(kv_weight, "pool", axis=1, tiled=True),
        preferred_element_type=jnp.float32,
    )
    fresh = lax.psum_scatter(partial_kv.astype(jnp.bfloat16), "tp", scatter_dimension=1, tiled=True)
    wanted = retrieval[0]
    npool = lax.axis_size("pool")
    by_token = lax.all_to_all(cache_table, "pool", split_axis=1, concat_axis=0, tiled=True)
    by_token = by_token.reshape(by_token.shape[0], by_token.shape[2])
    wanted_all = lax.all_gather(retrieval, "pool", axis=0, tiled=True)
    reply = jnp.take(by_token, wanted_all, axis=0)
    fetched = lax.all_to_all(
        reply[:, :, None, :], "pool", split_axis=0, concat_axis=2, tiled=True
    )[0]
    count = hidden_rows.shape[0]
    fetch_count = wanted.shape[0]
    group = QH // KVH
    scale = float(HD) ** (-0.5)
    local_heads = fresh.shape[1] // (2 * HD)
    width = fetched.shape[2]
    per_step = math.gcd(fetch_count, 8)
    steps_count = fetch_count // per_step
    grouped = fetched.reshape(steps_count, per_step * BLK, width)
    pat_steps = jnp.transpose(
        pattern[0].reshape(pattern.shape[1], steps_count, per_step), (1, 0, 2)
    )
    token_of_row = jnp.arange(count * group) // group
    block_of_row = token_of_row // RBLK
    row_blocks = block_of_row[:, None, None] == jnp.arange(pattern.shape[1])[None, :, None]
    near_mask = token_of_row[:, None] >= jnp.arange(count)[None, :]
    q_heads = queries.reshape(count, local_heads, group * HD)
    q_rows = q_heads[:, 0].reshape(count * group, HD)
    near_keys = fresh[:, 0:HD]
    near_vals = fresh[:, HD : 2 * HD]
    near_scores = rows_by_keys(q_rows, near_keys) * scale
    top = jnp.max(jnp.where(near_mask, near_scores, -1e30), axis=1)
    weights = jnp.where(near_mask, jnp.exp(near_scores - top[:, None]), 0.0)
    total = jnp.sum(weights, axis=1)
    numer = jnp.dot(weights.astype(jnp.bfloat16), near_vals, preferred_element_type=jnp.float32)

    def visit(carry, items):
        top_now, total_now, numer_now = carry
        block_rows, pat_now = items
        keys = block_rows[:, 0:HD]
        vals = block_rows[:, HD : 2 * HD]
        scores = rows_by_keys(q_rows, keys) * scale
        row_pat = jnp.any(row_blocks & (pat_now[None] != 0), axis=1)
        mask = jnp.repeat(row_pat, BLK, axis=1)
        top_new = jnp.maximum(top_now, jnp.max(jnp.where(mask, scores, -1e30), axis=1))
        weights_now = jnp.where(mask, jnp.exp(scores - top_new[:, None]), 0.0)
        factor = jnp.exp(top_now - top_new)
        total_new = total_now * factor + jnp.sum(weights_now, axis=1)
        numer_new = numer_now * factor[:, None] + jnp.dot(
            weights_now.astype(jnp.bfloat16), vals, preferred_element_type=jnp.float32
        )
        return ((top_new, total_new, numer_new), None)

    (top, total, numer), unused = lax.scan(visit, (top, total, numer), (grouped, pat_steps))
    results = (numer / total[:, None]).reshape(count, group * HD)
    attended = results.astype(jnp.bfloat16)
    return (attended, fresh)


def solution(mesh):
    placed = (
        P("pool", "tp"),
        P("tp", "pool"),
        P("pool", "tp"),
        P("pool", None, "tp"),
        P("pool", None),
        P("pool", None, None),
    )
    return jax.shard_map(
        body,
        mesh=mesh,
        in_specs=placed,
        out_specs=(P("pool", "tp"), P("pool", "tp")),
        check_vma=False,
    )
```

```python
import math

import jax
import jax.numpy as jnp
import numpy as np
from jax import lax
from jax.sharding import Mesh
from jax.sharding import PartitionSpec as P

HD = 128
QH = 32
KVH = 4
BLK = 128
RBLK = 64
CHIPS = ("px", "pz")
POOL = ("px", "pz", "pc")
ID_SPLIT = 32


def rows_by_keys(left, right):
    return lax.dot_general(
        left, right, (((1,), (1,)), ((), ())), preferred_element_type=jnp.float32
    )


def merge(carry, scores, mask, vals):
    top_now, total_now, numer_now = carry
    top_new = jnp.maximum(top_now, jnp.max(jnp.where(mask, scores, -1e30), axis=1))
    weights_now = jnp.where(mask, jnp.exp(scores - top_new[:, None]), 0.0)
    factor = jnp.exp(top_now - top_new)
    total_new = total_now * factor + jnp.sum(weights_now, axis=1)
    numer_new = numer_now * factor[:, None] + jnp.dot(
        weights_now.astype(jnp.bfloat16), vals, preferred_element_type=jnp.float32
    )
    return (top_new, total_new, numer_new)


def body(hidden_rows, kv_weight, queries, cache_table, retrieval, pattern):
    blocks_dev, blk, width = cache_table.shape
    npool = lax.axis_size(POOL)
    fetch_count = retrieval.shape[1]
    wanted = retrieval[0]
    id_row = jnp.concatenate(
        [
            (wanted // ID_SPLIT).astype(jnp.bfloat16),
            (wanted % ID_SPLIT).astype(jnp.bfloat16),
            jnp.zeros((width - 2 * fetch_count,), jnp.bfloat16),
        ]
    )
    id_block = jnp.broadcast_to(id_row[None, None, :], (1, blk, width))
    outgoing = jnp.concatenate([cache_table, id_block], axis=0)
    by_token = lax.all_to_all(outgoing, POOL, split_axis=1, concat_axis=0, tiled=True)
    by_token = by_token.reshape(npool, blocks_dev + 1, width)
    table = by_token[:, :blocks_dev].reshape(npool * blocks_dev, width)
    id_rows = by_token[:, blocks_dev].astype(jnp.float32)
    wanted_all = (
        id_rows[:, :fetch_count] * ID_SPLIT + id_rows[:, fetch_count : 2 * fetch_count]
    ).astype(jnp.int32)
    picks = (
        wanted_all.reshape(-1)[:, None]
        == jnp.arange(npool * blocks_dev, dtype=jnp.int32)[None, :]
    ).astype(jnp.bfloat16)
    reply = jnp.dot(picks, table, preferred_element_type=jnp.float32).astype(jnp.bfloat16)
    reply = reply.reshape(npool, fetch_count, 1, width)
    fetched = lax.all_to_all(reply, POOL, split_axis=0, concat_axis=2, tiled=True)[0]

    w_chip = lax.all_gather(kv_weight, CHIPS, axis=1, tiled=True)
    w_all = lax.all_gather(w_chip, "pc", axis=1, tiled=True)
    partial_kv = jnp.dot(hidden_rows, w_all, preferred_element_type=jnp.float32)
    ncore = lax.axis_size("pc")
    nchip = npool // ncore
    cols = kv_weight.shape[1]
    partial_kv = (
        partial_kv.reshape(-1, ncore, nchip, cols)
        .transpose(0, 2, 1, 3)
        .reshape(partial_kv.shape[0], -1)
    )
    fresh = lax.psum_scatter(partial_kv.astype(jnp.bfloat16), "tp", scatter_dimension=1, tiled=True)

    count = hidden_rows.shape[0]
    group = QH // KVH
    scale = float(HD) ** (-0.5)
    local_heads = fresh.shape[1] // (2 * HD)
    per_step = math.gcd(fetch_count, 8)
    steps_count = fetch_count // per_step
    grouped = fetched.reshape(steps_count, per_step * BLK, width)
    pat_steps = jnp.transpose(
        pattern[0].reshape(pattern.shape[1], steps_count, per_step), (1, 0, 2)
    )
    token_of_row = jnp.arange(count * group) // group
    block_of_row = token_of_row // RBLK
    row_blocks = block_of_row[:, None, None] == jnp.arange(pattern.shape[1])[None, :, None]
    near_mask = token_of_row[:, None] >= jnp.arange(count)[None, :]
    q_heads = queries.reshape(count, local_heads, group * HD)
    q_rows = q_heads[:, 0].reshape(count * group, HD)
    rows = count * group
    start = (
        jnp.full((rows,), -1e30, jnp.float32),
        jnp.zeros((rows,), jnp.float32),
        jnp.zeros((rows, HD), jnp.float32),
    )

    def visit(carry, items):
        block_rows, pat_now = items
        keys = block_rows[:, 0:HD]
        vals = block_rows[:, HD : 2 * HD]
        scores = rows_by_keys(q_rows, keys) * scale
        row_pat = jnp.any(row_blocks & (pat_now[None] != 0), axis=1)
        mask = jnp.repeat(row_pat, BLK, axis=1)
        return (merge(carry, scores, mask, vals), None)

    carry, unused = lax.scan(visit, start, (grouped, pat_steps))
    near_keys = fresh[:, 0:HD]
    near_vals = fresh[:, HD : 2 * HD]
    near_scores = rows_by_keys(q_rows, near_keys) * scale
    top, total, numer = merge(carry, near_scores, near_mask, near_vals)
    results = (numer / total[:, None]).reshape(count, group * HD)
    attended = results.astype(jnp.bfloat16)
    return (attended, fresh)


def solution(mesh):
    npool = mesh.shape["pool"]
    ntp = mesh.shape["tp"]
    nx = 4 if npool % 8 == 0 else 1
    fine = Mesh(
        np.asarray(mesh.devices).reshape(nx, npool // (2 * nx), 2, ntp),
        ("px", "pz", "pc", "tp"),
    )
    placed = (
        P(POOL, "tp"),
        P("tp", POOL),
        P(POOL, "tp"),
        P(POOL, None, "tp"),
        P(POOL, None),
        P(POOL, None, None),
    )
    return jax.shard_map(
        body,
        mesh=fine,
        in_specs=placed,
        out_specs=(P(POOL, "tp"), P(POOL, "tp")),
        check_vma=False,
    )
```

```python
import math

import jax
import jax.numpy as jnp
import numpy as np
from jax import lax
from jax.sharding import Mesh
from jax.sharding import PartitionSpec as P

HD = 128
QH = 32
KVH = 4
BLK = 128
RBLK = 64
CHIPS = ("px", "pz")
POOL = ("px", "pz", "pc")
ID_SPLIT = 32


def rows_by_keys(left, right):
    return lax.dot_general(
        left, right, (((1,), (1,)), ((), ())), preferred_element_type=jnp.float32
    )


def merge(carry, scores, mask, vals):
    top_now, total_now, numer_now = carry
    top_new = jnp.maximum(top_now, jnp.max(jnp.where(mask, scores, -1e30), axis=1))
    weights_now = jnp.where(mask, jnp.exp(scores - top_new[:, None]), 0.0)
    factor = jnp.exp(top_now - top_new)
    total_new = total_now * factor + jnp.sum(weights_now, axis=1)
    numer_new = numer_now * factor[:, None] + jnp.dot(
        weights_now.astype(jnp.bfloat16), vals, preferred_element_type=jnp.float32
    )
    return (top_new, total_new, numer_new)


def body(hidden_rows, kv_weight, queries, cache_table, retrieval, pattern):
    blocks_dev, blk, width = cache_table.shape
    npool = lax.axis_size(POOL)
    fetch_count = retrieval.shape[1]
    wanted = retrieval[0]
    id_row = jnp.concatenate(
        [
            (wanted // ID_SPLIT).astype(jnp.bfloat16),
            (wanted % ID_SPLIT).astype(jnp.bfloat16),
            jnp.zeros((width - 2 * fetch_count,), jnp.bfloat16),
        ]
    )
    id_block = jnp.broadcast_to(id_row[None, None, :], (1, blk, width))
    outgoing = jnp.concatenate([cache_table, id_block], axis=0)
    by_token = lax.all_to_all(outgoing, POOL, split_axis=1, concat_axis=0, tiled=True)
    by_token = by_token.reshape(npool, blocks_dev + 1, width)
    table = by_token[:, :blocks_dev].reshape(npool * blocks_dev, width)
    id_rows = by_token[:, blocks_dev].astype(jnp.float32)
    wanted_all = (
        id_rows[:, :fetch_count] * ID_SPLIT + id_rows[:, fetch_count : 2 * fetch_count]
    ).astype(jnp.int32)
    w_chip = lax.all_gather(kv_weight, CHIPS, axis=1, tiled=True)
    picks = (
        wanted_all.reshape(-1)[:, None]
        == jnp.arange(npool * blocks_dev, dtype=jnp.int32)[None, :]
    ).astype(jnp.bfloat16)
    reply = jnp.dot(picks, table, preferred_element_type=jnp.float32).astype(jnp.bfloat16)
    reply = reply.reshape(npool, fetch_count, 1, width)
    reply, w_chip = lax.optimization_barrier((reply, w_chip))
    fetched = lax.all_to_all(reply, POOL, split_axis=0, concat_axis=2, tiled=True)[0]

    w_all = lax.all_gather(w_chip, "pc", axis=1, tiled=True)
    partial_kv = jnp.dot(hidden_rows, w_all, preferred_element_type=jnp.float32)
    ncore = lax.axis_size("pc")
    nchip = npool // ncore
    cols = kv_weight.shape[1]
    partial_kv = (
        partial_kv.reshape(-1, ncore, nchip, cols)
        .transpose(0, 2, 1, 3)
        .reshape(partial_kv.shape[0], -1)
    )
    fresh = lax.psum_scatter(partial_kv.astype(jnp.bfloat16), "tp", scatter_dimension=1, tiled=True)

    count = hidden_rows.shape[0]
    group = QH // KVH
    scale = float(HD) ** (-0.5)
    local_heads = fresh.shape[1] // (2 * HD)
    per_step = math.gcd(fetch_count, 8)
    steps_count = fetch_count // per_step
    grouped = fetched.reshape(steps_count, per_step * BLK, width)
    pat_steps = jnp.transpose(
        pattern[0].reshape(pattern.shape[1], steps_count, per_step), (1, 0, 2)
    )
    token_of_row = jnp.arange(count * group) // group
    block_of_row = token_of_row // RBLK
    row_blocks = block_of_row[:, None, None] == jnp.arange(pattern.shape[1])[None, :, None]
    near_mask = token_of_row[:, None] >= jnp.arange(count)[None, :]
    q_heads = queries.reshape(count, local_heads, group * HD)
    q_rows = q_heads[:, 0].reshape(count * group, HD)
    near_keys = fresh[:, 0:HD]
    near_vals = fresh[:, HD : 2 * HD]
    near_scores = rows_by_keys(q_rows, near_keys) * scale
    top = jnp.max(jnp.where(near_mask, near_scores, -1e30), axis=1)
    weights = jnp.where(near_mask, jnp.exp(near_scores - top[:, None]), 0.0)
    total = jnp.sum(weights, axis=1)
    numer = jnp.dot(weights.astype(jnp.bfloat16), near_vals, preferred_element_type=jnp.float32)

    def visit(carry, items):
        block_rows, pat_now = items
        keys = block_rows[:, 0:HD]
        vals = block_rows[:, HD : 2 * HD]
        scores = rows_by_keys(q_rows, keys) * scale
        row_pat = jnp.any(row_blocks & (pat_now[None] != 0), axis=1)
        mask = jnp.repeat(row_pat, BLK, axis=1)
        return (merge(carry, scores, mask, vals), None)

    (top, total, numer), unused = lax.scan(visit, (top, total, numer), (grouped, pat_steps))
    results = (numer / total[:, None]).reshape(count, group * HD)
    attended = results.astype(jnp.bfloat16)
    return (attended, fresh)


def solution(mesh):
    npool = mesh.shape["pool"]
    ntp = mesh.shape["tp"]
    nx = 4 if npool % 8 == 0 else 1
    fine = Mesh(
        np.asarray(mesh.devices).reshape(nx, npool // (2 * nx), 2, ntp),
        ("px", "pz", "pc", "tp"),
    )
    placed = (
        P(POOL, "tp"),
        P("tp", POOL),
        P(POOL, "tp"),
        P(POOL, None, "tp"),
        P(POOL, None),
        P(POOL, None, None),
    )
    return jax.shard_map(
        body,
        mesh=fine,
        in_specs=placed,
        out_specs=(P(POOL, "tp"), P(POOL, "tp")),
        check_vma=False,
    )
```

```python
import math

import jax
import jax.numpy as jnp
import numpy as np
from jax import lax
from jax.sharding import Mesh
from jax.sharding import PartitionSpec as P

HD = 128
QH = 32
KVH = 4
BLK = 128
RBLK = 64
POOL = ("px", "pz", "pc")
ID_SPLIT = 32


def rows_by_keys(left, right):
    return lax.dot_general(
        left, right, (((1,), (1,)), ((), ())), preferred_element_type=jnp.float32
    )


def merge(carry, scores, mask, vals):
    top_now, total_now, numer_now = carry
    top_new = jnp.maximum(top_now, jnp.max(jnp.where(mask, scores, -1e30), axis=1))
    weights_now = jnp.where(mask, jnp.exp(scores - top_new[:, None]), 0.0)
    factor = jnp.exp(top_now - top_new)
    total_new = total_now * factor + jnp.sum(weights_now, axis=1)
    numer_new = numer_now * factor[:, None] + jnp.dot(
        weights_now.astype(jnp.bfloat16), vals, preferred_element_type=jnp.float32
    )
    return (top_new, total_new, numer_new)


def body(hidden_rows, kv_weight, queries, cache_table, retrieval, pattern):
    blocks_dev, blk, width = cache_table.shape
    npool = lax.axis_size(POOL)
    fetch_count = retrieval.shape[1]
    wanted = retrieval[0]
    id_row = jnp.concatenate(
        [
            (wanted // ID_SPLIT).astype(jnp.bfloat16),
            (wanted % ID_SPLIT).astype(jnp.bfloat16),
            jnp.zeros((width - 2 * fetch_count,), jnp.bfloat16),
        ]
    )
    id_block = jnp.broadcast_to(id_row[None, None, :], (1, blk, width))
    outgoing = jnp.concatenate([cache_table, id_block], axis=0)
    by_token = lax.all_to_all(outgoing, POOL, split_axis=1, concat_axis=0, tiled=True)
    by_token = by_token.reshape(npool, blocks_dev + 1, width)
    table = by_token[:, :blocks_dev].reshape(npool * blocks_dev, width)
    id_rows = by_token[:, blocks_dev].astype(jnp.float32)
    wanted_all = (
        id_rows[:, :fetch_count] * ID_SPLIT + id_rows[:, fetch_count : 2 * fetch_count]
    ).astype(jnp.int32)
    w_chip = lax.all_gather(kv_weight, "pz", axis=1, tiled=True)
    w_chip = lax.all_gather(w_chip, "px", axis=1, tiled=True)
    picks = (
        wanted_all.reshape(-1)[:, None]
        == jnp.arange(npool * blocks_dev, dtype=jnp.int32)[None, :]
    ).astype(jnp.bfloat16)
    reply = jnp.dot(picks, table, preferred_element_type=jnp.float32).astype(jnp.bfloat16)
    reply = reply.reshape(npool, fetch_count, 1, width)
    reply, w_chip = lax.optimization_barrier((reply, w_chip))
    fetched = lax.all_to_all(reply, POOL, split_axis=0, concat_axis=0, tiled=True)

    w_all = lax.all_gather(w_chip, "pc", axis=1, tiled=True)
    partial_kv = jnp.dot(hidden_rows, w_all, preferred_element_type=jnp.float32)
    ncore = lax.axis_size("pc")
    nchip = npool // ncore
    cols = kv_weight.shape[1]
    partial_kv = (
        partial_kv.reshape(-1, ncore, nchip, cols)
        .transpose(0, 2, 1, 3)
        .reshape(partial_kv.shape[0], -1)
    )
    fresh = lax.psum_scatter(partial_kv.astype(jnp.bfloat16), "tp", scatter_dimension=1, tiled=True)

    count = hidden_rows.shape[0]
    group = QH // KVH
    scale = float(HD) ** (-0.5)
    local_heads = fresh.shape[1] // (2 * HD)
    tokens_step = BLK // math.gcd(BLK, 8)
    steps_count = BLK // tokens_step
    grouped = fetched.reshape(steps_count, tokens_step * fetch_count, width)
    token_of_row = jnp.arange(count * group) // group
    block_of_row = token_of_row // RBLK
    row_pat = jnp.take(pattern[0] != 0, block_of_row, axis=0)
    mask = jnp.tile(row_pat, (1, tokens_step))
    near_mask = token_of_row[:, None] >= jnp.arange(count)[None, :]
    q_heads = queries.reshape(count, local_heads, group * HD)
    q_rows = q_heads[:, 0].reshape(count * group, HD)
    near_keys = fresh[:, 0:HD]
    near_vals = fresh[:, HD : 2 * HD]
    near_scores = rows_by_keys(q_rows, near_keys) * scale
    top = jnp.max(jnp.where(near_mask, near_scores, -1e30), axis=1)
    weights = jnp.where(near_mask, jnp.exp(near_scores - top[:, None]), 0.0)
    total = jnp.sum(weights, axis=1)
    numer = jnp.dot(weights.astype(jnp.bfloat16), near_vals, preferred_element_type=jnp.float32)

    def visit(carry, block_rows):
        keys = block_rows[:, 0:HD]
        vals = block_rows[:, HD : 2 * HD]
        scores = rows_by_keys(q_rows, keys) * scale
        return (merge(carry, scores, mask, vals), None)

    (top, total, numer), unused = lax.scan(visit, (top, total, numer), grouped)
    results = (numer / total[:, None]).reshape(count, group * HD)
    attended = results.astype(jnp.bfloat16)
    return (attended, fresh)


def solution(mesh):
    npool = mesh.shape["pool"]
    ntp = mesh.shape["tp"]
    nx = 4 if npool % 8 == 0 else 1
    fine = Mesh(
        np.asarray(mesh.devices).reshape(nx, npool // (2 * nx), 2, ntp),
        ("px", "pz", "pc", "tp"),
    )
    placed = (
        P(POOL, "tp"),
        P("tp", POOL),
        P(POOL, "tp"),
        P(POOL, None, "tp"),
        P(POOL, None),
        P(POOL, None, None),
    )
    return jax.shard_map(
        body,
        mesh=fine,
        in_specs=placed,
        out_specs=(P(POOL, "tp"), P(POOL, "tp")),
        check_vma=False,
    )
```

```python
import math

import jax
import jax.numpy as jnp
import numpy as np
from jax import lax
from jax.sharding import Mesh
from jax.sharding import PartitionSpec as P

HD = 128
QH = 32
KVH = 4
BLK = 128
RBLK = 64
POOL = ("px", "pz", "pc")
ID_SPLIT = 32


def rows_by_keys(left, right):
    return lax.dot_general(
        left, right, (((1,), (1,)), ((), ())), preferred_element_type=jnp.float32
    )


def merge(carry, scores, mask, vals):
    top_now, total_now, numer_now = carry
    top_new = jnp.maximum(top_now, jnp.max(jnp.where(mask, scores, -1e30), axis=1))
    weights_now = jnp.where(mask, jnp.exp(scores - top_new[:, None]), 0.0)
    factor = jnp.exp(top_now - top_new)
    total_new = total_now * factor + jnp.sum(weights_now, axis=1)
    numer_new = numer_now * factor[:, None] + jnp.dot(
        weights_now.astype(jnp.bfloat16), vals, preferred_element_type=jnp.float32
    )
    return (top_new, total_new, numer_new)


def body(hidden_rows, kv_weight, queries, cache_table, retrieval, pattern):
    blocks_dev, blk, width = cache_table.shape
    npool = lax.axis_size(POOL)
    fetch_count = retrieval.shape[1]
    wanted = retrieval[0]
    id_row = jnp.concatenate(
        [
            (wanted // ID_SPLIT).astype(jnp.bfloat16),
            (wanted % ID_SPLIT).astype(jnp.bfloat16),
            jnp.zeros((width - 2 * fetch_count,), jnp.bfloat16),
        ]
    )
    id_block = jnp.broadcast_to(id_row[None, None, :], (1, blk, width))
    outgoing = jnp.concatenate([cache_table, id_block], axis=0)
    by_token = lax.all_to_all(outgoing, POOL, split_axis=1, concat_axis=0, tiled=True)
    by_token = by_token.reshape(npool, blocks_dev + 1, width)
    table = by_token[:, :blocks_dev].reshape(npool * blocks_dev, width)
    id_rows = by_token[:, blocks_dev].astype(jnp.float32)
    wanted_all = (
        id_rows[:, :fetch_count] * ID_SPLIT + id_rows[:, fetch_count : 2 * fetch_count]
    ).astype(jnp.int32)
    nz = lax.axis_size("pz")
    w_z = kv_weight
    dist = 1
    while dist < nz:
        perm = [(i, (i - dist) % nz) for i in range(nz)]
        w_z = jnp.concatenate([w_z, lax.ppermute(w_z, "pz", perm)], axis=1)
        dist *= 2
    picks = (
        wanted_all.reshape(-1)[:, None]
        == jnp.arange(npool * blocks_dev, dtype=jnp.int32)[None, :]
    ).astype(jnp.bfloat16)
    reply = jnp.dot(picks, table, preferred_element_type=jnp.float32).astype(jnp.bfloat16)
    reply = reply.reshape(npool, fetch_count, 1, width)
    reply, w_z = lax.optimization_barrier((reply, w_z))
    fetched = lax.all_to_all(reply, POOL, split_axis=0, concat_axis=0, tiled=True)

    w_chip = lax.all_gather(w_z, "px", axis=1, tiled=True)
    w_all = lax.all_gather(w_chip, "pc", axis=1, tiled=True)
    partial_kv = jnp.dot(hidden_rows, w_all, preferred_element_type=jnp.float32)
    ncore = lax.axis_size("pc")
    nx = lax.axis_size("px")
    cols = kv_weight.shape[1]
    partial_kv = partial_kv.reshape(-1, ncore, nx, nz, cols)
    partial_kv = jnp.roll(partial_kv, lax.axis_index("pz"), axis=3)
    partial_kv = partial_kv.transpose(0, 2, 3, 1, 4).reshape(partial_kv.shape[0], -1)
    fresh = lax.psum_scatter(partial_kv.astype(jnp.bfloat16), "tp", scatter_dimension=1, tiled=True)

    count = hidden_rows.shape[0]
    group = QH // KVH
    scale = float(HD) ** (-0.5)
    local_heads = fresh.shape[1] // (2 * HD)
    tokens_step = BLK // math.gcd(BLK, 8)
    steps_count = BLK // tokens_step
    grouped = fetched.reshape(steps_count, tokens_step * fetch_count, width)
    token_of_row = jnp.arange(count * group) // group
    block_of_row = token_of_row // RBLK
    row_pat = jnp.take(pattern[0] != 0, block_of_row, axis=0)
    mask = jnp.tile(row_pat, (1, tokens_step))
    near_mask = token_of_row[:, None] >= jnp.arange(count)[None, :]
    q_heads = queries.reshape(count, local_heads, group * HD)
    q_rows = q_heads[:, 0].reshape(count * group, HD)
    near_keys = fresh[:, 0:HD]
    near_vals = fresh[:, HD : 2 * HD]
    near_scores = rows_by_keys(q_rows, near_keys) * scale
    top = jnp.max(jnp.where(near_mask, near_scores, -1e30), axis=1)
    weights = jnp.where(near_mask, jnp.exp(near_scores - top[:, None]), 0.0)
    total = jnp.sum(weights, axis=1)
    numer = jnp.dot(weights.astype(jnp.bfloat16), near_vals, preferred_element_type=jnp.float32)

    def visit(carry, block_rows):
        keys = block_rows[:, 0:HD]
        vals = block_rows[:, HD : 2 * HD]
        scores = rows_by_keys(q_rows, keys) * scale
        return (merge(carry, scores, mask, vals), None)

    (top, total, numer), unused = lax.scan(visit, (top, total, numer), grouped)
    results = (numer / total[:, None]).reshape(count, group * HD)
    attended = results.astype(jnp.bfloat16)
    return (attended, fresh)


def solution(mesh):
    npool = mesh.shape["pool"]
    ntp = mesh.shape["tp"]
    nx = 4 if npool % 8 == 0 else 1
    fine = Mesh(
        np.asarray(mesh.devices).reshape(nx, npool // (2 * nx), 2, ntp),
        ("px", "pz", "pc", "tp"),
    )
    placed = (
        P(POOL, "tp"),
        P("tp", POOL),
        P(POOL, "tp"),
        P(POOL, None, "tp"),
        P(POOL, None),
        P(POOL, None, None),
    )
    return jax.shard_map(
        body,
        mesh=fine,
        in_specs=placed,
        out_specs=(P(POOL, "tp"), P(POOL, "tp")),
        check_vma=False,
    )
```

```python
import math

import jax
import jax.numpy as jnp
import numpy as np
from jax import lax
from jax.sharding import Mesh
from jax.sharding import PartitionSpec as P

HD = 128
QH = 32
KVH = 4
BLK = 128
RBLK = 64
POOL = ("px", "pz", "pc")
ID_SPLIT = 32


def rows_by_keys(left, right):
    return lax.dot_general(
        left, right, (((1,), (1,)), ((), ())), preferred_element_type=jnp.float32
    )


def merge(carry, scores, mask, vals):
    top_now, total_now, numer_now = carry
    top_new = jnp.maximum(top_now, jnp.max(jnp.where(mask, scores, -1e30), axis=1))
    weights_now = jnp.where(mask, jnp.exp(scores - top_new[:, None]), 0.0)
    factor = jnp.exp(top_now - top_new)
    total_new = total_now * factor + jnp.sum(weights_now, axis=1)
    numer_new = numer_now * factor[:, None] + jnp.dot(
        weights_now.astype(jnp.bfloat16), vals, preferred_element_type=jnp.float32
    )
    return (top_new, total_new, numer_new)


def body(hidden_rows, kv_weight, queries, cache_table, retrieval, pattern):
    blocks_dev, blk, width = cache_table.shape
    npool = lax.axis_size(POOL)
    fetch_count = retrieval.shape[1]
    wanted = retrieval[0]
    id_row = jnp.concatenate(
        [
            (wanted // ID_SPLIT).astype(jnp.bfloat16),
            (wanted % ID_SPLIT).astype(jnp.bfloat16),
            jnp.zeros((width - 2 * fetch_count,), jnp.bfloat16),
        ]
    )
    id_block = jnp.broadcast_to(id_row[None, None, :], (1, blk, width))
    outgoing = jnp.concatenate([cache_table, id_block], axis=0)
    by_token = lax.all_to_all(outgoing, POOL, split_axis=1, concat_axis=0, tiled=True)
    by_token = by_token.reshape(npool, blocks_dev + 1, width)
    table = by_token[:, :blocks_dev].reshape(npool * blocks_dev, width)
    id_rows = by_token[:, blocks_dev].astype(jnp.float32)
    wanted_all = (
        id_rows[:, :fetch_count] * ID_SPLIT + id_rows[:, fetch_count : 2 * fetch_count]
    ).astype(jnp.int32)
    picks = (
        wanted_all.reshape(-1)[:, None]
        == jnp.arange(npool * blocks_dev, dtype=jnp.int32)[None, :]
    ).astype(jnp.bfloat16)
    reply = jnp.dot(picks, table, preferred_element_type=jnp.float32).astype(jnp.bfloat16)
    reply = reply.reshape(npool, fetch_count, 1, width)
    fetched = lax.all_to_all(reply, POOL, split_axis=0, concat_axis=0, tiled=True)

    w_head = lax.all_gather(kv_weight, ("pz", "pc"), axis=1, tiled=True)
    h_ring = lax.all_gather(hidden_rows, "px", axis=0, tiled=False)
    part = jnp.einsum("xrd,dc->xrc", h_ring, w_head, preferred_element_type=jnp.float32)
    part = lax.all_to_all(part.astype(jnp.bfloat16), "px", split_axis=0, concat_axis=0, tiled=True)
    partial_kv = part.transpose(1, 0, 2).reshape(part.shape[1], -1)
    fresh = lax.psum_scatter(partial_kv, "tp", scatter_dimension=1, tiled=True)

    count = hidden_rows.shape[0]
    group = QH // KVH
    scale = float(HD) ** (-0.5)
    local_heads = fresh.shape[1] // (2 * HD)
    tokens_step = BLK // math.gcd(BLK, 8)
    steps_count = BLK // tokens_step
    grouped = fetched.reshape(steps_count, tokens_step * fetch_count, width)
    token_of_row = jnp.arange(count * group) // group
    block_of_row = token_of_row // RBLK
    row_pat = jnp.take(pattern[0] != 0, block_of_row, axis=0)
    mask = jnp.tile(row_pat, (1, tokens_step))
    near_mask = token_of_row[:, None] >= jnp.arange(count)[None, :]
    q_heads = queries.reshape(count, local_heads, group * HD)
    q_rows = q_heads[:, 0].reshape(count * group, HD)
    near_keys = fresh[:, 0:HD]
    near_vals = fresh[:, HD : 2 * HD]
    near_scores = rows_by_keys(q_rows, near_keys) * scale
    top = jnp.max(jnp.where(near_mask, near_scores, -1e30), axis=1)
    weights = jnp.where(near_mask, jnp.exp(near_scores - top[:, None]), 0.0)
    total = jnp.sum(weights, axis=1)
    numer = jnp.dot(weights.astype(jnp.bfloat16), near_vals, preferred_element_type=jnp.float32)

    def visit(carry, block_rows):
        keys = block_rows[:, 0:HD]
        vals = block_rows[:, HD : 2 * HD]
        scores = rows_by_keys(q_rows, keys) * scale
        return (merge(carry, scores, mask, vals), None)

    (top, total, numer), unused = lax.scan(visit, (top, total, numer), grouped)
    results = (numer / total[:, None]).reshape(count, group * HD)
    attended = results.astype(jnp.bfloat16)
    return (attended, fresh)


def solution(mesh):
    npool = mesh.shape["pool"]
    ntp = mesh.shape["tp"]
    nx = 4 if npool % 8 == 0 else 1
    fine = Mesh(
        np.asarray(mesh.devices).reshape(nx, npool // (2 * nx), 2, ntp),
        ("px", "pz", "pc", "tp"),
    )
    placed = (
        P(POOL, "tp"),
        P("tp", POOL),
        P(POOL, "tp"),
        P(POOL, None, "tp"),
        P(POOL, None),
        P(POOL, None, None),
    )
    return jax.shard_map(
        body,
        mesh=fine,
        in_specs=placed,
        out_specs=(P(POOL, "tp"), P(POOL, "tp")),
        check_vma=False,
    )
```

```python
import math

import jax
import jax.numpy as jnp
import numpy as np
from jax import lax
from jax.sharding import Mesh
from jax.sharding import PartitionSpec as P

HD = 128
QH = 32
KVH = 4
BLK = 128
RBLK = 64
POOL = ("px", "pz", "pc")
ID_SPLIT = 32


def rows_by_keys(left, right):
    return lax.dot_general(
        left, right, (((1,), (1,)), ((), ())), preferred_element_type=jnp.float32
    )


def merge(carry, scores, mask, vals):
    top_now, total_now, numer_now = carry
    top_new = jnp.maximum(top_now, jnp.max(jnp.where(mask, scores, -1e30), axis=1))
    weights_now = jnp.where(mask, jnp.exp(scores - top_new[:, None]), 0.0)
    factor = jnp.exp(top_now - top_new)
    total_new = total_now * factor + jnp.sum(weights_now, axis=1)
    numer_new = numer_now * factor[:, None] + jnp.dot(
        weights_now.astype(jnp.bfloat16), vals, preferred_element_type=jnp.float32
    )
    return (top_new, total_new, numer_new)


def body(hidden_rows, kv_weight, queries, cache_table, retrieval, pattern):
    blocks_dev, blk, width = cache_table.shape
    npool = lax.axis_size(POOL)
    fetch_count = retrieval.shape[1]
    wanted = retrieval[0]
    id_row = jnp.concatenate(
        [
            (wanted // ID_SPLIT).astype(jnp.bfloat16),
            (wanted % ID_SPLIT).astype(jnp.bfloat16),
            jnp.zeros((width - 2 * fetch_count,), jnp.bfloat16),
        ]
    )
    id_block = jnp.broadcast_to(id_row[None, None, :], (1, blk, width))
    outgoing = jnp.concatenate([cache_table, id_block], axis=0)
    by_token = lax.all_to_all(outgoing, POOL, split_axis=1, concat_axis=0, tiled=True)
    by_token = by_token.reshape(npool, blocks_dev + 1, width)
    table = by_token[:, :blocks_dev].reshape(npool * blocks_dev, width)
    id_rows = by_token[:, blocks_dev].astype(jnp.float32)
    wanted_all = (
        id_rows[:, :fetch_count] * ID_SPLIT + id_rows[:, fetch_count : 2 * fetch_count]
    ).astype(jnp.int32)
    picks = (
        wanted_all.reshape(-1)[:, None]
        == jnp.arange(npool * blocks_dev, dtype=jnp.int32)[None, :]
    ).astype(jnp.bfloat16)
    reply = jnp.dot(picks, table, preferred_element_type=jnp.float32).astype(jnp.bfloat16)
    reply = reply.reshape(npool, fetch_count, 1, width)
    reply, hidden_rows, kv_weight = lax.optimization_barrier((reply, hidden_rows, kv_weight))
    fetched = lax.all_to_all(reply, POOL, split_axis=0, concat_axis=0, tiled=True)

    w_head = lax.all_gather(kv_weight, ("pz", "pc"), axis=1, tiled=True)
    h_ring = lax.all_gather(hidden_rows, "px", axis=0, tiled=False)
    part = jnp.einsum("xrd,dc->xrc", h_ring, w_head, preferred_element_type=jnp.float32)
    ntp = lax.axis_size("tp")
    head_slot = jnp.arange(ntp) == lax.axis_index("px")
    spread = jnp.where(
        head_slot[None, :, None, None], part.astype(jnp.bfloat16)[:, None], jnp.zeros((), jnp.bfloat16)
    )
    spread = spread.reshape(-1, part.shape[1], part.shape[2])
    fresh = lax.psum_scatter(spread, ("px", "tp"), scatter_dimension=0, tiled=True)[0]

    count = hidden_rows.shape[0]
    group = QH // KVH
    scale = float(HD) ** (-0.5)
    local_heads = fresh.shape[1] // (2 * HD)
    tokens_step = BLK // math.gcd(BLK, 8)
    steps_count = BLK // tokens_step
    grouped = fetched.reshape(steps_count, tokens_step * fetch_count, width)
    token_of_row = jnp.arange(count * group) // group
    block_of_row = token_of_row // RBLK
    row_pat = jnp.take(pattern[0] != 0, block_of_row, axis=0)
    mask = jnp.tile(row_pat, (1, tokens_step))
    near_mask = token_of_row[:, None] >= jnp.arange(count)[None, :]
    q_heads = queries.reshape(count, local_heads, group * HD)
    q_rows = q_heads[:, 0].reshape(count * group, HD)
    near_keys = fresh[:, 0:HD]
    near_vals = fresh[:, HD : 2 * HD]
    near_scores = rows_by_keys(q_rows, near_keys) * scale
    top = jnp.max(jnp.where(near_mask, near_scores, -1e30), axis=1)
    weights = jnp.where(near_mask, jnp.exp(near_scores - top[:, None]), 0.0)
    total = jnp.sum(weights, axis=1)
    numer = jnp.dot(weights.astype(jnp.bfloat16), near_vals, preferred_element_type=jnp.float32)

    def visit(carry, block_rows):
        keys = block_rows[:, 0:HD]
        vals = block_rows[:, HD : 2 * HD]
        scores = rows_by_keys(q_rows, keys) * scale
        return (merge(carry, scores, mask, vals), None)

    (top, total, numer), unused = lax.scan(visit, (top, total, numer), grouped)
    results = (numer / total[:, None]).reshape(count, group * HD)
    attended = results.astype(jnp.bfloat16)
    return (attended, fresh)


def solution(mesh):
    npool = mesh.shape["pool"]
    ntp = mesh.shape["tp"]
    nx = 4 if npool % 8 == 0 else 1
    fine = Mesh(
        np.asarray(mesh.devices).reshape(nx, npool // (2 * nx), 2, ntp),
        ("px", "pz", "pc", "tp"),
    )
    placed = (
        P(POOL, "tp"),
        P("tp", POOL),
        P(POOL, "tp"),
        P(POOL, None, "tp"),
        P(POOL, None),
        P(POOL, None, None),
    )
    return jax.shard_map(
        body,
        mesh=fine,
        in_specs=placed,
        out_specs=(P(POOL, "tp"), P(POOL, "tp")),
        check_vma=False,
    )
```

```python
import math

import jax
import jax.numpy as jnp
import numpy as np
from jax import lax
from jax.sharding import Mesh
from jax.sharding import PartitionSpec as P

HD = 128
QH = 32
KVH = 4
BLK = 128
RBLK = 64
POOL = ("px", "pz", "pc")
ID_SPLIT = 32


def rows_by_keys(left, right):
    return lax.dot_general(
        left, right, (((1,), (1,)), ((), ())), preferred_element_type=jnp.float32
    )


def merge(carry, scores, mask, vals):
    top_now, total_now, numer_now = carry
    top_new = jnp.maximum(top_now, jnp.max(jnp.where(mask, scores, -1e30), axis=1))
    weights_now = jnp.where(mask, jnp.exp(scores - top_new[:, None]), 0.0)
    factor = jnp.exp(top_now - top_new)
    total_new = total_now * factor + jnp.sum(weights_now, axis=1)
    numer_new = numer_now * factor[:, None] + jnp.dot(
        weights_now.astype(jnp.bfloat16), vals, preferred_element_type=jnp.float32
    )
    return (top_new, total_new, numer_new)


def body(hidden_rows, kv_weight, queries, cache_table, retrieval, pattern):
    blocks_dev, blk, width = cache_table.shape
    npool = lax.axis_size(POOL)
    fetch_count = retrieval.shape[1]
    wanted = retrieval[0]
    id_row = jnp.concatenate(
        [
            (wanted // ID_SPLIT).astype(jnp.bfloat16),
            (wanted % ID_SPLIT).astype(jnp.bfloat16),
            jnp.zeros((width - 2 * fetch_count,), jnp.bfloat16),
        ]
    )
    id_block = jnp.broadcast_to(id_row[None, None, :], (1, blk, width))
    outgoing = jnp.concatenate([cache_table, id_block], axis=0)
    by_token = lax.all_to_all(outgoing, POOL, split_axis=1, concat_axis=0, tiled=True)
    by_token = by_token.reshape(npool, blocks_dev + 1, width)
    table = by_token[:, :blocks_dev].reshape(npool * blocks_dev, width)
    id_rows = by_token[:, blocks_dev].astype(jnp.float32)
    wanted_all = (
        id_rows[:, :fetch_count] * ID_SPLIT + id_rows[:, fetch_count : 2 * fetch_count]
    ).astype(jnp.int32)
    picks = (
        wanted_all.reshape(-1)[:, None]
        == jnp.arange(npool * blocks_dev, dtype=jnp.int32)[None, :]
    ).astype(jnp.bfloat16)
    reply = jnp.dot(picks, table, preferred_element_type=jnp.float32).astype(jnp.bfloat16)
    reply = reply.reshape(npool, fetch_count, 1, width)
    reply, hidden_rows, kv_weight = lax.optimization_barrier((reply, hidden_rows, kv_weight))
    fetched = lax.all_to_all(reply, POOL, split_axis=0, concat_axis=0, tiled=True)

    w_head = lax.all_gather(kv_weight, ("pz", "pc"), axis=1, tiled=True)
    h_ring = lax.all_gather(hidden_rows, "px", axis=0, tiled=False)
    part = jnp.einsum("xrd,dc->xrc", h_ring, w_head, preferred_element_type=jnp.float32)
    ntp = lax.axis_size("tp")
    head_slot = jnp.arange(ntp) == lax.axis_index("px")
    spread = jnp.where(
        head_slot[None, :, None, None], part.astype(jnp.bfloat16)[:, None], jnp.zeros((), jnp.bfloat16)
    )
    moved = lax.psum_scatter(spread, "px", scatter_dimension=0, tiled=True)
    fresh = lax.psum_scatter(moved[0], "tp", scatter_dimension=0, tiled=True)[0]

    count = hidden_rows.shape[0]
    group = QH // KVH
    scale = float(HD) ** (-0.5)
    local_heads = fresh.shape[1] // (2 * HD)
    tokens_step = BLK // math.gcd(BLK, 8)
    steps_count = BLK // tokens_step
    grouped = fetched.reshape(steps_count, tokens_step * fetch_count, width)
    token_of_row = jnp.arange(count * group) // group
    block_of_row = token_of_row // RBLK
    row_pat = jnp.take(pattern[0] != 0, block_of_row, axis=0)
    mask = jnp.tile(row_pat, (1, tokens_step))
    near_mask = token_of_row[:, None] >= jnp.arange(count)[None, :]
    q_heads = queries.reshape(count, local_heads, group * HD)
    q_rows = q_heads[:, 0].reshape(count * group, HD)
    rows = count * group
    start = (
        jnp.full((rows,), -1e30, jnp.float32),
        jnp.zeros((rows,), jnp.float32),
        jnp.zeros((rows, HD), jnp.float32),
    )

    def visit(carry, block_rows):
        keys = block_rows[:, 0:HD]
        vals = block_rows[:, HD : 2 * HD]
        scores = rows_by_keys(q_rows, keys) * scale
        return (merge(carry, scores, mask, vals), None)

    carry, unused = lax.scan(visit, start, grouped)
    near_keys = fresh[:, 0:HD]
    near_vals = fresh[:, HD : 2 * HD]
    near_scores = rows_by_keys(q_rows, near_keys) * scale
    top, total, numer = merge(carry, near_scores, near_mask, near_vals)
    results = (numer / total[:, None]).reshape(count, group * HD)
    attended = results.astype(jnp.bfloat16)
    return (attended, fresh)


def solution(mesh):
    npool = mesh.shape["pool"]
    ntp = mesh.shape["tp"]
    nx = 4 if npool % 8 == 0 else 1
    fine = Mesh(
        np.asarray(mesh.devices).reshape(nx, npool // (2 * nx), 2, ntp),
        ("px", "pz", "pc", "tp"),
    )
    placed = (
        P(POOL, "tp"),
        P("tp", POOL),
        P(POOL, "tp"),
        P(POOL, None, "tp"),
        P(POOL, None),
        P(POOL, None, None),
    )
    return jax.shard_map(
        body,
        mesh=fine,
        in_specs=placed,
        out_specs=(P(POOL, "tp"), P(POOL, "tp")),
        check_vma=False,
    )
```

```python
import math

import jax
import jax.numpy as jnp
import numpy as np
from jax import lax
from jax.sharding import Mesh
from jax.sharding import PartitionSpec as P

HD = 128
QH = 32
KVH = 4
BLK = 128
RBLK = 64
POOL = ("px", "pz", "pc")
ID_SPLIT = 32


def rows_by_keys(left, right):
    return lax.dot_general(
        left, right, (((1,), (1,)), ((), ())), preferred_element_type=jnp.float32
    )


def merge(carry, scores, mask, vals):
    top_now, total_now, numer_now = carry
    top_new = jnp.maximum(top_now, jnp.max(jnp.where(mask, scores, -1e30), axis=1))
    weights_now = jnp.where(mask, jnp.exp(scores - top_new[:, None]), 0.0)
    factor = jnp.exp(top_now - top_new)
    total_new = total_now * factor + jnp.sum(weights_now, axis=1)
    numer_new = numer_now * factor[:, None] + jnp.dot(
        weights_now.astype(jnp.bfloat16), vals, preferred_element_type=jnp.float32
    )
    return (top_new, total_new, numer_new)


def body(hidden_rows, kv_weight, queries, cache_table, retrieval, pattern):
    blocks_dev, blk, width = cache_table.shape
    npool = lax.axis_size(POOL)
    fetch_count = retrieval.shape[1]
    wanted = retrieval[0]
    id_row = jnp.concatenate(
        [
            (wanted // ID_SPLIT).astype(jnp.bfloat16),
            (wanted % ID_SPLIT).astype(jnp.bfloat16),
            jnp.zeros((width - 2 * fetch_count,), jnp.bfloat16),
        ]
    )
    id_block = jnp.broadcast_to(id_row[None, None, :], (1, blk, width))
    outgoing = jnp.concatenate([cache_table, id_block], axis=0)
    by_token = lax.all_to_all(outgoing, POOL, split_axis=1, concat_axis=0, tiled=True)
    by_token = by_token.reshape(npool, blocks_dev + 1, width)
    table = by_token[:, :blocks_dev].reshape(npool * blocks_dev, width)
    id_rows = by_token[:, blocks_dev].astype(jnp.float32)
    wanted_all = (
        id_rows[:, :fetch_count] * ID_SPLIT + id_rows[:, fetch_count : 2 * fetch_count]
    ).astype(jnp.int32)
    picks = (
        wanted_all.reshape(-1)[:, None]
        == jnp.arange(npool * blocks_dev, dtype=jnp.int32)[None, :]
    ).astype(jnp.bfloat16)
    reply = jnp.dot(picks, table, preferred_element_type=jnp.float32).astype(jnp.bfloat16)
    reply = reply.reshape(npool, fetch_count, 1, width)
    reply, hidden_rows, kv_weight = lax.optimization_barrier((reply, hidden_rows, kv_weight))
    fetched = lax.all_to_all(reply, POOL, split_axis=0, concat_axis=0, tiled=True)

    w_head = lax.all_gather(kv_weight, ("pz", "pc"), axis=1, tiled=True)
    h_ring = lax.all_gather(hidden_rows, "px", axis=0, tiled=False)
    part = jnp.einsum("xrd,dc->xrc", h_ring, w_head, preferred_element_type=jnp.float32)
    ntp = lax.axis_size("tp")
    head_slot = jnp.arange(ntp) == lax.axis_index("px")
    spread = jnp.where(
        head_slot[None, :, None, None], part.astype(jnp.bfloat16)[:, None], jnp.zeros((), jnp.bfloat16)
    )
    moved = lax.psum_scatter(spread, "px", scatter_dimension=0, tiled=True)
    fresh = lax.psum_scatter(moved[0], "tp", scatter_dimension=0, tiled=True)[0]

    count = hidden_rows.shape[0]
    group = QH // KVH
    scale = float(HD) ** (-0.5)
    local_heads = fresh.shape[1] // (2 * HD)
    tokens_step = BLK // math.gcd(BLK, 8)
    steps_count = BLK // tokens_step
    grouped = fetched.reshape(steps_count, tokens_step * fetch_count, width)
    token_of_row = jnp.arange(count * group) // group
    block_of_row = token_of_row // RBLK
    row_pat = jnp.take(pattern[0] != 0, block_of_row, axis=0)
    mask = jnp.tile(row_pat, (1, tokens_step))
    near_mask = token_of_row[:, None] >= jnp.arange(count)[None, :]
    q_heads = queries.reshape(count, local_heads, group * HD)
    q_rows = q_heads[:, 0].reshape(count * group, HD)
    near_keys = fresh[:, 0:HD]
    near_vals = fresh[:, HD : 2 * HD]
    near_scores = rows_by_keys(q_rows, near_keys) * scale
    top = jnp.max(jnp.where(near_mask, near_scores, -1e30), axis=1)
    weights = jnp.where(near_mask, jnp.exp(near_scores - top[:, None]), 0.0)
    total = jnp.sum(weights, axis=1)
    numer = jnp.dot(weights.astype(jnp.bfloat16), near_vals, preferred_element_type=jnp.float32)

    def visit(carry, block_rows):
        keys = block_rows[:, 0:HD]
        vals = block_rows[:, HD : 2 * HD]
        scores = rows_by_keys(q_rows, keys) * scale
        return (merge(carry, scores, mask, vals), None)

    (top, total, numer), unused = lax.scan(visit, (top, total, numer), grouped)
    results = (numer / total[:, None]).reshape(count, group * HD)
    attended = results.astype(jnp.bfloat16)
    return (attended, fresh)


def solution(mesh):
    npool = mesh.shape["pool"]
    ntp = mesh.shape["tp"]
    nx = 4 if npool % 8 == 0 else 1
    fine = Mesh(
        np.asarray(mesh.devices).reshape(nx, npool // (2 * nx), 2, ntp),
        ("px", "pz", "pc", "tp"),
    )
    placed = (
        P(POOL, "tp"),
        P("tp", POOL),
        P(POOL, "tp"),
        P(POOL, None, "tp"),
        P(POOL, None),
        P(POOL, None, None),
    )
    return jax.shard_map(
        body,
        mesh=fine,
        in_specs=placed,
        out_specs=(P(POOL, "tp"), P(POOL, "tp")),
        check_vma=False,
    )
```

```python
import math

import jax
import jax.numpy as jnp
import numpy as np
from jax import lax
from jax.sharding import Mesh
from jax.sharding import PartitionSpec as P

HD = 128
QH = 32
KVH = 4
BLK = 128
RBLK = 64
POOL = ("px", "pz", "pc")
ID_SPLIT = 32


def rows_by_keys(left, right):
    return lax.dot_general(
        left, right, (((1,), (1,)), ((), ())), preferred_element_type=jnp.float32
    )


def merge(carry, scores, mask, vals):
    top_now, total_now, numer_now = carry
    top_new = jnp.maximum(top_now, jnp.max(jnp.where(mask, scores, -1e30), axis=1))
    weights_now = jnp.where(mask, jnp.exp(scores - top_new[:, None]), 0.0)
    factor = jnp.exp(top_now - top_new)
    total_new = total_now * factor + jnp.sum(weights_now, axis=1)
    numer_new = numer_now * factor[:, None] + jnp.dot(
        weights_now.astype(jnp.bfloat16), vals, preferred_element_type=jnp.float32
    )
    return (top_new, total_new, numer_new)


def body(hidden_rows, kv_weight, queries, cache_table, retrieval, pattern):
    blocks_dev, blk, width = cache_table.shape
    npool = lax.axis_size(POOL)
    fetch_count = retrieval.shape[1]
    wanted = retrieval[0]
    id_row = jnp.concatenate(
        [
            (wanted // ID_SPLIT).astype(jnp.bfloat16),
            (wanted % ID_SPLIT).astype(jnp.bfloat16),
            jnp.zeros((width - 2 * fetch_count,), jnp.bfloat16),
        ]
    )
    id_block = jnp.broadcast_to(id_row[None, None, :], (1, blk, width))
    outgoing = jnp.concatenate([cache_table, id_block], axis=0)
    nx, nz, nc = (lax.axis_size(a) for a in POOL)
    rows_out = blocks_dev + 1
    step = outgoing.reshape(rows_out, nx, nz, nc, width)
    step = lax.all_to_all(step, "pz", split_axis=2, concat_axis=2, tiled=True)
    step = step.transpose(0, 1, 3, 2, 4).reshape(rows_out, nx * nc, nz, width)
    step = lax.all_to_all(step, ("px", "pc"), split_axis=1, concat_axis=1, tiled=True)
    step = step.reshape(rows_out, nx, nc, nz, width).transpose(1, 3, 2, 0, 4)
    by_token = step.reshape(npool, rows_out, width)
    table = by_token[:, :blocks_dev].reshape(npool * blocks_dev, width)
    id_rows = by_token[:, blocks_dev].astype(jnp.float32)
    wanted_all = (
        id_rows[:, :fetch_count] * ID_SPLIT + id_rows[:, fetch_count : 2 * fetch_count]
    ).astype(jnp.int32)
    picks = (
        wanted_all.reshape(-1)[:, None]
        == jnp.arange(npool * blocks_dev, dtype=jnp.int32)[None, :]
    ).astype(jnp.bfloat16)
    reply = jnp.dot(picks, table, preferred_element_type=jnp.float32).astype(jnp.bfloat16)
    reply = reply.reshape(npool, fetch_count, 1, width)
    reply, hidden_rows, kv_weight = lax.optimization_barrier((reply, hidden_rows, kv_weight))
    fetched = lax.all_to_all(reply, POOL, split_axis=0, concat_axis=0, tiled=True)

    w_head = lax.all_gather(kv_weight, ("pz", "pc"), axis=1, tiled=True)
    h_ring = lax.all_gather(hidden_rows, "px", axis=0, tiled=False)
    part = jnp.einsum("xrd,dc->xrc", h_ring, w_head, preferred_element_type=jnp.float32)
    ntp = lax.axis_size("tp")
    head_slot = jnp.arange(ntp) == lax.axis_index("px")
    spread = jnp.where(
        head_slot[None, :, None, None], part.astype(jnp.bfloat16)[:, None], jnp.zeros((), jnp.bfloat16)
    )
    moved = lax.psum_scatter(spread, "px", scatter_dimension=0, tiled=True)
    fresh = lax.psum_scatter(moved[0], "tp", scatter_dimension=0, tiled=True)[0]

    count = hidden_rows.shape[0]
    group = QH // KVH
    scale = float(HD) ** (-0.5)
    local_heads = fresh.shape[1] // (2 * HD)
    tokens_step = BLK // math.gcd(BLK, 8)
    steps_count = BLK // tokens_step
    grouped = fetched.reshape(steps_count, tokens_step * fetch_count, width)
    token_of_row = jnp.arange(count * group) // group
    block_of_row = token_of_row // RBLK
    row_pat = jnp.take(pattern[0] != 0, block_of_row, axis=0)
    mask = jnp.tile(row_pat, (1, tokens_step))
    near_mask = token_of_row[:, None] >= jnp.arange(count)[None, :]
    q_heads = queries.reshape(count, local_heads, group * HD)
    q_rows = q_heads[:, 0].reshape(count * group, HD)
    near_keys = fresh[:, 0:HD]
    near_vals = fresh[:, HD : 2 * HD]
    near_scores = rows_by_keys(q_rows, near_keys) * scale
    top = jnp.max(jnp.where(near_mask, near_scores, -1e30), axis=1)
    weights = jnp.where(near_mask, jnp.exp(near_scores - top[:, None]), 0.0)
    total = jnp.sum(weights, axis=1)
    numer = jnp.dot(weights.astype(jnp.bfloat16), near_vals, preferred_element_type=jnp.float32)

    def visit(carry, block_rows):
        keys = block_rows[:, 0:HD]
        vals = block_rows[:, HD : 2 * HD]
        scores = rows_by_keys(q_rows, keys) * scale
        return (merge(carry, scores, mask, vals), None)

    (top, total, numer), unused = lax.scan(visit, (top, total, numer), grouped)
    results = (numer / total[:, None]).reshape(count, group * HD)
    attended = results.astype(jnp.bfloat16)
    return (attended, fresh)


def solution(mesh):
    npool = mesh.shape["pool"]
    ntp = mesh.shape["tp"]
    nx = 4 if npool % 8 == 0 else 1
    fine = Mesh(
        np.asarray(mesh.devices).reshape(nx, npool // (2 * nx), 2, ntp),
        ("px", "pz", "pc", "tp"),
    )
    placed = (
        P(POOL, "tp"),
        P("tp", POOL),
        P(POOL, "tp"),
        P(POOL, None, "tp"),
        P(POOL, None),
        P(POOL, None, None),
    )
    return jax.shard_map(
        body,
        mesh=fine,
        in_specs=placed,
        out_specs=(P(POOL, "tp"), P(POOL, "tp")),
        check_vma=False,
    )
```

```python
import math

import jax
import jax.numpy as jnp
import numpy as np
from jax import lax
from jax.sharding import Mesh
from jax.sharding import PartitionSpec as P

HD = 128
QH = 32
KVH = 4
BLK = 128
RBLK = 64
POOL = ("px", "pz", "pc")
ID_SPLIT = 32


def rows_by_keys(left, right):
    return lax.dot_general(
        left, right, (((1,), (1,)), ((), ())), preferred_element_type=jnp.float32
    )


def merge(carry, scores, mask, vals):
    top_now, total_now, numer_now = carry
    top_new = jnp.maximum(top_now, jnp.max(jnp.where(mask, scores, -1e30), axis=1))
    weights_now = jnp.where(mask, jnp.exp(scores - top_new[:, None]), 0.0)
    factor = jnp.exp(top_now - top_new)
    total_new = total_now * factor + jnp.sum(weights_now, axis=1)
    numer_new = numer_now * factor[:, None] + jnp.dot(
        weights_now.astype(jnp.bfloat16), vals, preferred_element_type=jnp.float32
    )
    return (top_new, total_new, numer_new)


def body(hidden_rows, kv_weight, queries, cache_table, retrieval, pattern):
    blocks_dev, blk, width = cache_table.shape
    npool = lax.axis_size(POOL)
    fetch_count = retrieval.shape[1]
    wanted = retrieval[0]
    id_row = jnp.concatenate(
        [
            (wanted // ID_SPLIT).astype(jnp.bfloat16),
            (wanted % ID_SPLIT).astype(jnp.bfloat16),
            jnp.zeros((width - 2 * fetch_count,), jnp.bfloat16),
        ]
    )
    id_block = jnp.broadcast_to(id_row[None, None, :], (1, blk, width))
    outgoing = jnp.concatenate([cache_table, id_block], axis=0)
    nx, nz, nc = (lax.axis_size(a) for a in POOL)
    rows_out = blocks_dev + 1
    step = outgoing.reshape(rows_out, nx, nz, nc, width)
    step = lax.all_to_all(step, "pz", split_axis=2, concat_axis=2, tiled=True)
    step = step.transpose(0, 1, 3, 2, 4).reshape(rows_out, nx * nc, nz, width)
    step = lax.all_to_all(step, ("px", "pc"), split_axis=1, concat_axis=1, tiled=True)
    step = step.reshape(rows_out, nx, nc, nz, width).transpose(1, 3, 2, 0, 4)
    by_token = step.reshape(npool, rows_out, width)
    table = by_token[:, :blocks_dev].reshape(npool * blocks_dev, width)
    id_rows = by_token[:, blocks_dev].astype(jnp.float32)
    wanted_all = (
        id_rows[:, :fetch_count] * ID_SPLIT + id_rows[:, fetch_count : 2 * fetch_count]
    ).astype(jnp.int32)
    picks = (
        wanted_all.reshape(-1)[:, None]
        == jnp.arange(npool * blocks_dev, dtype=jnp.int32)[None, :]
    ).astype(jnp.bfloat16)
    reply = jnp.dot(picks, table, preferred_element_type=jnp.float32).astype(jnp.bfloat16)
    reply = reply.reshape(npool, fetch_count, 1, width)
    reply, hidden_rows, kv_weight = lax.optimization_barrier((reply, hidden_rows, kv_weight))
    fetched = lax.all_to_all(reply, POOL, split_axis=0, concat_axis=0, tiled=True)

    w_head = lax.all_gather(kv_weight, ("pz", "pc"), axis=1, tiled=True)
    h_ring = lax.all_gather(hidden_rows, "px", axis=0, tiled=False)
    part = jnp.einsum("xrd,dc->xrc", h_ring, w_head, preferred_element_type=jnp.float32)
    ntp = lax.axis_size("tp")
    head_slot = jnp.arange(ntp) == lax.axis_index("px")
    spread = jnp.where(
        head_slot[None, :, None, None], part.astype(jnp.bfloat16)[:, None], jnp.zeros((), jnp.bfloat16)
    )
    moved = lax.psum_scatter(spread, "px", scatter_dimension=0, tiled=True)
    fresh = lax.psum_scatter(moved[0], "tp", scatter_dimension=0, tiled=True)[0]

    count = hidden_rows.shape[0]
    group = QH // KVH
    scale = float(HD) ** (-0.5)
    local_heads = fresh.shape[1] // (2 * HD)
    tokens_step = BLK // math.gcd(BLK, 8)
    steps_count = BLK // tokens_step
    grouped = fetched.reshape(steps_count, tokens_step * fetch_count, width)
    token_of_row = jnp.arange(count * group) // group
    block_of_row = token_of_row // RBLK
    row_pat = jnp.take(pattern[0] != 0, block_of_row, axis=0)
    mask = jnp.tile(row_pat, (1, tokens_step))
    near_mask = token_of_row[:, None] >= jnp.arange(count)[None, :]
    q_heads = queries.reshape(count, local_heads, group * HD)
    q_rows = q_heads[:, 0].reshape(count * group, HD)
    near_keys = fresh[:, 0:HD]
    near_vals = fresh[:, HD : 2 * HD]
    near_scores = rows_by_keys(q_rows, near_keys) * scale
    top = jnp.max(jnp.where(near_mask, near_scores, -1e30), axis=1)
    weights = jnp.where(near_mask, jnp.exp(near_scores - top[:, None]), 0.0)
    total = jnp.sum(weights, axis=1)
    numer = jnp.dot(weights.astype(jnp.bfloat16), near_vals, preferred_element_type=jnp.float32)

    def visit(carry, block_rows):
        keys = block_rows[:, 0:HD]
        vals = block_rows[:, HD : 2 * HD]
        scores = rows_by_keys(q_rows, keys) * scale
        return (merge(carry, scores, mask, vals), None)

    (top, total, numer), unused = lax.scan(visit, (top, total, numer), grouped, unroll=True)
    results = (numer / total[:, None]).reshape(count, group * HD)
    attended = results.astype(jnp.bfloat16)
    return (attended, fresh)


def solution(mesh):
    npool = mesh.shape["pool"]
    ntp = mesh.shape["tp"]
    nx = 4 if npool % 8 == 0 else 1
    fine = Mesh(
        np.asarray(mesh.devices).reshape(nx, npool // (2 * nx), 2, ntp),
        ("px", "pz", "pc", "tp"),
    )
    placed = (
        P(POOL, "tp"),
        P("tp", POOL),
        P(POOL, "tp"),
        P(POOL, None, "tp"),
        P(POOL, None),
        P(POOL, None, None),
    )
    return jax.shard_map(
        body,
        mesh=fine,
        in_specs=placed,
        out_specs=(P(POOL, "tp"), P(POOL, "tp")),
        check_vma=False,
    )
```

```python
import math

import jax
import jax.numpy as jnp
import numpy as np
from jax import lax
from jax.sharding import Mesh
from jax.sharding import PartitionSpec as P

HD = 128
QH = 32
KVH = 4
BLK = 128
RBLK = 64
POOL = ("px", "pz", "pc")
ID_SPLIT = 32


def rows_by_keys(left, right):
    return lax.dot_general(
        left, right, (((1,), (1,)), ((), ())), preferred_element_type=jnp.float32
    )


def merge(carry, scores, mask, vals):
    top_now, total_now, numer_now = carry
    top_new = jnp.maximum(top_now, jnp.max(jnp.where(mask, scores, -1e30), axis=1))
    weights_now = jnp.where(mask, jnp.exp(scores - top_new[:, None]), 0.0)
    factor = jnp.exp(top_now - top_new)
    total_new = total_now * factor + jnp.sum(weights_now, axis=1)
    numer_new = numer_now * factor[:, None] + jnp.dot(
        weights_now.astype(jnp.bfloat16), vals, preferred_element_type=jnp.float32
    )
    return (top_new, total_new, numer_new)


def body(hidden_rows, kv_weight, queries, cache_table, retrieval, pattern):
    blocks_dev, blk, width = cache_table.shape
    npool = lax.axis_size(POOL)
    fetch_count = retrieval.shape[1]
    wanted = retrieval[0]
    id_row = jnp.concatenate(
        [
            (wanted // ID_SPLIT).astype(jnp.bfloat16),
            (wanted % ID_SPLIT).astype(jnp.bfloat16),
            jnp.zeros((width - 2 * fetch_count,), jnp.bfloat16),
        ]
    )
    id_block = jnp.broadcast_to(id_row[None, None, :], (1, blk, width))
    outgoing = jnp.concatenate([cache_table, id_block], axis=0)
    nx, nz, nc = (lax.axis_size(a) for a in POOL)
    rows_out = blocks_dev + 1
    step = outgoing.reshape(rows_out, nx, nz, nc, width)
    step = lax.all_to_all(step, "pz", split_axis=2, concat_axis=2, tiled=True)
    step = step.transpose(0, 1, 3, 2, 4).reshape(rows_out, nx * nc, nz, width)
    step = lax.all_to_all(step, ("px", "pc"), split_axis=1, concat_axis=1, tiled=True)
    step = step.reshape(rows_out, nx, nc, nz, width).transpose(1, 3, 2, 0, 4)
    by_token = step.reshape(npool, rows_out, width)
    table = by_token[:, :blocks_dev].reshape(npool * blocks_dev, width)
    id_rows = by_token[:, blocks_dev].astype(jnp.float32)
    wanted_all = (
        id_rows[:, :fetch_count] * ID_SPLIT + id_rows[:, fetch_count : 2 * fetch_count]
    ).astype(jnp.int32)
    picks = (
        wanted_all.reshape(-1)[:, None]
        == jnp.arange(npool * blocks_dev, dtype=jnp.int32)[None, :]
    ).astype(jnp.bfloat16)
    reply = jnp.dot(picks, table, preferred_element_type=jnp.float32).astype(jnp.bfloat16)
    reply = reply.reshape(npool, fetch_count, 1, width)
    reply, hidden_rows, kv_weight = lax.optimization_barrier((reply, hidden_rows, kv_weight))
    fetched = lax.all_to_all(reply, POOL, split_axis=0, concat_axis=0, tiled=True)

    w_head = lax.all_gather(kv_weight, ("pz", "pc"), axis=1, tiled=True)
    w_all = lax.all_gather(w_head, "px", axis=1, tiled=True)
    partial_kv = jnp.dot(hidden_rows, w_all, preferred_element_type=jnp.float32)
    fresh = lax.psum_scatter(partial_kv.astype(jnp.bfloat16), "tp", scatter_dimension=1, tiled=True)

    count = hidden_rows.shape[0]
    group = QH // KVH
    scale = float(HD) ** (-0.5)
    local_heads = fresh.shape[1] // (2 * HD)
    tokens_step = BLK // math.gcd(BLK, 8)
    steps_count = BLK // tokens_step
    grouped = fetched.reshape(steps_count, tokens_step * fetch_count, width)
    token_of_row = jnp.arange(count * group) // group
    block_of_row = token_of_row // RBLK
    row_pat = jnp.take(pattern[0] != 0, block_of_row, axis=0)
    mask = jnp.tile(row_pat, (1, tokens_step))
    near_mask = token_of_row[:, None] >= jnp.arange(count)[None, :]
    q_heads = queries.reshape(count, local_heads, group * HD)
    q_rows = q_heads[:, 0].reshape(count * group, HD)
    near_keys = fresh[:, 0:HD]
    near_vals = fresh[:, HD : 2 * HD]
    near_scores = rows_by_keys(q_rows, near_keys) * scale
    top = jnp.max(jnp.where(near_mask, near_scores, -1e30), axis=1)
    weights = jnp.where(near_mask, jnp.exp(near_scores - top[:, None]), 0.0)
    total = jnp.sum(weights, axis=1)
    numer = jnp.dot(weights.astype(jnp.bfloat16), near_vals, preferred_element_type=jnp.float32)

    def visit(carry, block_rows):
        keys = block_rows[:, 0:HD]
        vals = block_rows[:, HD : 2 * HD]
        scores = rows_by_keys(q_rows, keys) * scale
        return (merge(carry, scores, mask, vals), None)

    (top, total, numer), unused = lax.scan(visit, (top, total, numer), grouped)
    results = (numer / total[:, None]).reshape(count, group * HD)
    attended = results.astype(jnp.bfloat16)
    return (attended, fresh)


def solution(mesh):
    npool = mesh.shape["pool"]
    ntp = mesh.shape["tp"]
    nx = 4 if npool % 8 == 0 else 1
    fine = Mesh(
        np.asarray(mesh.devices).reshape(nx, npool // (2 * nx), 2, ntp),
        ("px", "pz", "pc", "tp"),
    )
    placed = (
        P(POOL, "tp"),
        P("tp", POOL),
        P(POOL, "tp"),
        P(POOL, None, "tp"),
        P(POOL, None),
        P(POOL, None, None),
    )
    return jax.shard_map(
        body,
        mesh=fine,
        in_specs=placed,
        out_specs=(P(POOL, "tp"), P(POOL, "tp")),
        check_vma=False,
    )
```

```python
import math

import jax
import jax.numpy as jnp
import numpy as np
from jax import lax
from jax.sharding import Mesh
from jax.sharding import PartitionSpec as P

HD = 128
QH = 32
KVH = 4
BLK = 128
RBLK = 64
POOL = ("px", "pz", "pc")
ID_SPLIT = 32


def rows_by_keys(left, right):
    return lax.dot_general(
        left, right, (((1,), (1,)), ((), ())), preferred_element_type=jnp.float32
    )


def merge(carry, scores, mask, vals):
    top_now, total_now, numer_now = carry
    top_new = jnp.maximum(top_now, jnp.max(jnp.where(mask, scores, -1e30), axis=1))
    weights_now = jnp.where(mask, jnp.exp(scores - top_new[:, None]), 0.0)
    factor = jnp.exp(top_now - top_new)
    total_new = total_now * factor + jnp.sum(weights_now, axis=1)
    numer_new = numer_now * factor[:, None] + jnp.dot(
        weights_now.astype(jnp.bfloat16), vals, preferred_element_type=jnp.float32
    )
    return (top_new, total_new, numer_new)


def body(hidden_rows, kv_weight, queries, cache_table, retrieval, pattern):
    blocks_dev, blk, width = cache_table.shape
    npool = lax.axis_size(POOL)
    fetch_count = retrieval.shape[1]
    wanted = retrieval[0]
    id_row = jnp.concatenate(
        [
            (wanted // ID_SPLIT).astype(jnp.bfloat16),
            (wanted % ID_SPLIT).astype(jnp.bfloat16),
            jnp.zeros((width - 2 * fetch_count,), jnp.bfloat16),
        ]
    )
    id_block = jnp.broadcast_to(id_row[None, None, :], (1, blk, width))
    outgoing = jnp.concatenate([cache_table, id_block], axis=0)
    nx, nz, nc = (lax.axis_size(a) for a in POOL)
    rows_out = blocks_dev + 1
    lanes = 128
    step = outgoing.reshape(rows_out, nx, nz, nc, width).transpose(2, 0, 1, 3, 4)
    step = step.reshape(nz, -1, lanes)
    step = lax.all_to_all(step, "pz", split_axis=0, concat_axis=0, tiled=True)
    step = step.reshape(nz, rows_out, nx, nc, width).transpose(2, 3, 0, 1, 4)
    step = step.reshape(nx * nc, -1, lanes)
    step = lax.all_to_all(step, ("px", "pc"), split_axis=0, concat_axis=0, tiled=True)
    step = step.reshape(nx, nc, nz, rows_out, width).transpose(0, 2, 1, 3, 4)
    by_token = step.reshape(npool, rows_out, width)
    table = by_token[:, :blocks_dev].reshape(npool * blocks_dev, width)
    id_rows = by_token[:, blocks_dev].astype(jnp.float32)
    wanted_all = (
        id_rows[:, :fetch_count] * ID_SPLIT + id_rows[:, fetch_count : 2 * fetch_count]
    ).astype(jnp.int32)
    picks = (
        wanted_all.reshape(-1)[:, None]
        == jnp.arange(npool * blocks_dev, dtype=jnp.int32)[None, :]
    ).astype(jnp.bfloat16)
    reply = jnp.dot(picks, table, preferred_element_type=jnp.float32).astype(jnp.bfloat16)
    reply = reply.reshape(npool, fetch_count, 1, width)
    reply, hidden_rows, kv_weight = lax.optimization_barrier((reply, hidden_rows, kv_weight))
    fetched = lax.all_to_all(reply, POOL, split_axis=0, concat_axis=0, tiled=True)

    w_head = lax.all_gather(kv_weight, ("pz", "pc"), axis=1, tiled=True)
    w_all = lax.all_gather(w_head, "px", axis=1, tiled=True)
    partial_kv = jnp.dot(hidden_rows, w_all, preferred_element_type=jnp.float32)
    fresh = lax.psum_scatter(partial_kv.astype(jnp.bfloat16), "tp", scatter_dimension=1, tiled=True)

    count = hidden_rows.shape[0]
    group = QH // KVH
    scale = float(HD) ** (-0.5)
    local_heads = fresh.shape[1] // (2 * HD)
    tokens_step = BLK // math.gcd(BLK, 8)
    steps_count = BLK // tokens_step
    grouped = fetched.reshape(steps_count, tokens_step * fetch_count, width)
    token_of_row = jnp.arange(count * group) // group
    block_of_row = token_of_row // RBLK
    row_pat = jnp.take(pattern[0] != 0, block_of_row, axis=0)
    mask = jnp.tile(row_pat, (1, tokens_step))
    near_mask = token_of_row[:, None] >= jnp.arange(count)[None, :]
    q_heads = queries.reshape(count, local_heads, group * HD)
    q_rows = q_heads[:, 0].reshape(count * group, HD)
    near_keys = fresh[:, 0:HD]
    near_vals = fresh[:, HD : 2 * HD]
    near_scores = rows_by_keys(q_rows, near_keys) * scale
    top = jnp.max(jnp.where(near_mask, near_scores, -1e30), axis=1)
    weights = jnp.where(near_mask, jnp.exp(near_scores - top[:, None]), 0.0)
    total = jnp.sum(weights, axis=1)
    numer = jnp.dot(weights.astype(jnp.bfloat16), near_vals, preferred_element_type=jnp.float32)

    def visit(carry, block_rows):
        keys = block_rows[:, 0:HD]
        vals = block_rows[:, HD : 2 * HD]
        scores = rows_by_keys(q_rows, keys) * scale
        return (merge(carry, scores, mask, vals), None)

    (top, total, numer), unused = lax.scan(visit, (top, total, numer), grouped)
    results = (numer / total[:, None]).reshape(count, group * HD)
    attended = results.astype(jnp.bfloat16)
    return (attended, fresh)


def solution(mesh):
    npool = mesh.shape["pool"]
    ntp = mesh.shape["tp"]
    nx = 4 if npool % 8 == 0 else 1
    fine = Mesh(
        np.asarray(mesh.devices).reshape(nx, npool // (2 * nx), 2, ntp),
        ("px", "pz", "pc", "tp"),
    )
    placed = (
        P(POOL, "tp"),
        P("tp", POOL),
        P(POOL, "tp"),
        P(POOL, None, "tp"),
        P(POOL, None),
        P(POOL, None, None),
    )
    return jax.shard_map(
        body,
        mesh=fine,
        in_specs=placed,
        out_specs=(P(POOL, "tp"), P(POOL, "tp")),
        check_vma=False,
    )
```

```python
import math

import jax
import jax.numpy as jnp
import numpy as np
from jax import lax
from jax.sharding import Mesh
from jax.sharding import PartitionSpec as P

HD = 128
QH = 32
KVH = 4
BLK = 128
RBLK = 64
POOL = ("px", "pz", "pc")
ID_SPLIT = 32


def rows_by_keys(left, right):
    return lax.dot_general(
        left, right, (((1,), (1,)), ((), ())), preferred_element_type=jnp.float32
    )


def merge(carry, scores, mask, vals):
    top_now, total_now, numer_now = carry
    top_new = jnp.maximum(top_now, jnp.max(jnp.where(mask, scores, -1e30), axis=1))
    weights_now = jnp.where(mask, jnp.exp(scores - top_new[:, None]), 0.0)
    factor = jnp.exp(top_now - top_new)
    total_new = total_now * factor + jnp.sum(weights_now, axis=1)
    numer_new = numer_now * factor[:, None] + jnp.dot(
        weights_now.astype(jnp.bfloat16), vals, preferred_element_type=jnp.float32
    )
    return (top_new, total_new, numer_new)


def body(hidden_rows, kv_weight, queries, cache_table, retrieval, pattern):
    blocks_dev, blk, width = cache_table.shape
    npool = lax.axis_size(POOL)
    fetch_count = retrieval.shape[1]
    wanted = retrieval[0]
    id_row = jnp.concatenate(
        [
            (wanted // ID_SPLIT).astype(jnp.bfloat16),
            (wanted % ID_SPLIT).astype(jnp.bfloat16),
            jnp.zeros((width - 2 * fetch_count,), jnp.bfloat16),
        ]
    )
    id_block = jnp.broadcast_to(id_row[None, None, :], (1, blk, width))
    outgoing = jnp.concatenate([cache_table, id_block], axis=0)
    nx, nz, nc = (lax.axis_size(a) for a in POOL)
    rows_out = blocks_dev + 1
    step = outgoing.reshape(rows_out, nx, nz, nc, width).transpose(0, 1, 3, 2, 4)
    step = step.reshape(rows_out, nx * nc, nz, width)
    step = lax.all_to_all(step, ("px", "pc"), split_axis=1, concat_axis=1, tiled=True)
    step = lax.all_to_all(step, "pz", split_axis=2, concat_axis=2, tiled=True)
    step = step.reshape(rows_out, nx, nc, nz, width).transpose(1, 3, 2, 0, 4)
    by_token = step.reshape(npool, rows_out, width)
    table = by_token[:, :blocks_dev].reshape(npool * blocks_dev, width)
    id_rows = by_token[:, blocks_dev].astype(jnp.float32)
    wanted_all = (
        id_rows[:, :fetch_count] * ID_SPLIT + id_rows[:, fetch_count : 2 * fetch_count]
    ).astype(jnp.int32)
    picks = (
        wanted_all.reshape(-1)[:, None]
        == jnp.arange(npool * blocks_dev, dtype=jnp.int32)[None, :]
    ).astype(jnp.bfloat16)
    reply = jnp.dot(picks, table, preferred_element_type=jnp.float32).astype(jnp.bfloat16)
    reply = reply.reshape(npool, fetch_count, 1, width)
    reply, hidden_rows, kv_weight = lax.optimization_barrier((reply, hidden_rows, kv_weight))
    fetched = lax.all_to_all(reply, POOL, split_axis=0, concat_axis=0, tiled=True)

    w_head = lax.all_gather(kv_weight, ("pz", "pc"), axis=1, tiled=True)
    w_all = lax.all_gather(w_head, "px", axis=1, tiled=True)
    partial_kv = jnp.dot(hidden_rows, w_all, preferred_element_type=jnp.float32)
    fresh = lax.psum_scatter(partial_kv.astype(jnp.bfloat16), "tp", scatter_dimension=1, tiled=True)

    count = hidden_rows.shape[0]
    group = QH // KVH
    scale = float(HD) ** (-0.5)
    local_heads = fresh.shape[1] // (2 * HD)
    tokens_step = BLK // math.gcd(BLK, 8)
    steps_count = BLK // tokens_step
    grouped = fetched.reshape(steps_count, tokens_step * fetch_count, width)
    token_of_row = jnp.arange(count * group) // group
    block_of_row = token_of_row // RBLK
    row_pat = jnp.take(pattern[0] != 0, block_of_row, axis=0)
    mask = jnp.tile(row_pat, (1, tokens_step))
    near_mask = token_of_row[:, None] >= jnp.arange(count)[None, :]
    q_heads = queries.reshape(count, local_heads, group * HD)
    q_rows = q_heads[:, 0].reshape(count * group, HD)
    near_keys = fresh[:, 0:HD]
    near_vals = fresh[:, HD : 2 * HD]
    near_scores = rows_by_keys(q_rows, near_keys) * scale
    top = jnp.max(jnp.where(near_mask, near_scores, -1e30), axis=1)
    weights = jnp.where(near_mask, jnp.exp(near_scores - top[:, None]), 0.0)
    total = jnp.sum(weights, axis=1)
    numer = jnp.dot(weights.astype(jnp.bfloat16), near_vals, preferred_element_type=jnp.float32)

    def visit(carry, block_rows):
        keys = block_rows[:, 0:HD]
        vals = block_rows[:, HD : 2 * HD]
        scores = rows_by_keys(q_rows, keys) * scale
        return (merge(carry, scores, mask, vals), None)

    (top, total, numer), unused = lax.scan(visit, (top, total, numer), grouped)
    results = (numer / total[:, None]).reshape(count, group * HD)
    attended = results.astype(jnp.bfloat16)
    return (attended, fresh)


def solution(mesh):
    npool = mesh.shape["pool"]
    ntp = mesh.shape["tp"]
    nx = 4 if npool % 8 == 0 else 1
    fine = Mesh(
        np.asarray(mesh.devices).reshape(nx, npool // (2 * nx), 2, ntp),
        ("px", "pz", "pc", "tp"),
    )
    placed = (
        P(POOL, "tp"),
        P("tp", POOL),
        P(POOL, "tp"),
        P(POOL, None, "tp"),
        P(POOL, None),
        P(POOL, None, None),
    )
    return jax.shard_map(
        body,
        mesh=fine,
        in_specs=placed,
        out_specs=(P(POOL, "tp"), P(POOL, "tp")),
        check_vma=False,
    )
```

```python
import math

import jax
import jax.numpy as jnp
import numpy as np
from jax import lax
from jax.sharding import Mesh
from jax.sharding import PartitionSpec as P

HD = 128
QH = 32
KVH = 4
BLK = 128
RBLK = 64
POOL = ("px", "pzh", "pzl", "pc")
Z_AXES = ("pzh", "pzl")
ID_SPLIT = 32


def rows_by_keys(left, right):
    return lax.dot_general(
        left, right, (((1,), (1,)), ((), ())), preferred_element_type=jnp.float32
    )


def merge(carry, scores, mask, vals):
    top_now, total_now, numer_now = carry
    top_new = jnp.maximum(top_now, jnp.max(jnp.where(mask, scores, -1e30), axis=1))
    weights_now = jnp.where(mask, jnp.exp(scores - top_new[:, None]), 0.0)
    factor = jnp.exp(top_now - top_new)
    total_new = total_now * factor + jnp.sum(weights_now, axis=1)
    numer_new = numer_now * factor[:, None] + jnp.dot(
        weights_now.astype(jnp.bfloat16), vals, preferred_element_type=jnp.float32
    )
    return (top_new, total_new, numer_new)


def body(hidden_rows, kv_weight, queries, cache_table, retrieval, pattern):
    blocks_dev, blk, width = cache_table.shape
    npool = lax.axis_size(POOL)
    fetch_count = retrieval.shape[1]
    wanted = retrieval[0]
    id_row = jnp.concatenate(
        [
            (wanted // ID_SPLIT).astype(jnp.bfloat16),
            (wanted % ID_SPLIT).astype(jnp.bfloat16),
            jnp.zeros((width - 2 * fetch_count,), jnp.bfloat16),
        ]
    )
    id_block = jnp.broadcast_to(id_row[None, None, :], (1, blk, width))
    outgoing = jnp.concatenate([cache_table, id_block], axis=0)
    nx, nzh, nzl, nc = (lax.axis_size(a) for a in POOL)
    rows_out = blocks_dev + 1
    step = outgoing.reshape(rows_out, nx, nzh, nzl, nc, width).transpose(0, 1, 4, 2, 3, 5)
    step = step.reshape(rows_out, nx * nc, nzh, nzl, width)
    step = lax.all_to_all(step, ("px", "pc"), split_axis=1, concat_axis=1, tiled=True)
    step = lax.all_to_all(step, "pzl", split_axis=3, concat_axis=3, tiled=True)
    step = lax.all_to_all(step, "pzh", split_axis=2, concat_axis=2, tiled=True)
    step = step.reshape(rows_out, nx, nc, nzh, nzl, width).transpose(1, 3, 4, 2, 0, 5)
    by_token = step.reshape(npool, rows_out, width)
    table = by_token[:, :blocks_dev].reshape(npool * blocks_dev, width)
    id_rows = by_token[:, blocks_dev].astype(jnp.float32)
    wanted_all = (
        id_rows[:, :fetch_count] * ID_SPLIT + id_rows[:, fetch_count : 2 * fetch_count]
    ).astype(jnp.int32)
    picks = (
        wanted_all.reshape(-1)[:, None]
        == jnp.arange(npool * blocks_dev, dtype=jnp.int32)[None, :]
    ).astype(jnp.bfloat16)
    reply = jnp.dot(picks, table, preferred_element_type=jnp.float32).astype(jnp.bfloat16)
    reply = reply.reshape(npool, fetch_count, 1, width)
    reply, hidden_rows, kv_weight = lax.optimization_barrier((reply, hidden_rows, kv_weight))
    fetched = lax.all_to_all(reply, POOL, split_axis=0, concat_axis=0, tiled=True)

    w_head = lax.all_gather(kv_weight, Z_AXES + ("pc",), axis=1, tiled=True)
    w_all = lax.all_gather(w_head, "px", axis=1, tiled=True)
    partial_kv = jnp.dot(hidden_rows, w_all, preferred_element_type=jnp.float32)
    fresh = lax.psum_scatter(partial_kv.astype(jnp.bfloat16), "tp", scatter_dimension=1, tiled=True)

    count = hidden_rows.shape[0]
    group = QH // KVH
    scale = float(HD) ** (-0.5)
    local_heads = fresh.shape[1] // (2 * HD)
    tokens_step = BLK // math.gcd(BLK, 8)
    steps_count = BLK // tokens_step
    grouped = fetched.reshape(steps_count, tokens_step * fetch_count, width)
    token_of_row = jnp.arange(count * group) // group
    block_of_row = token_of_row // RBLK
    row_pat = jnp.take(pattern[0] != 0, block_of_row, axis=0)
    mask = jnp.tile(row_pat, (1, tokens_step))
    near_mask = token_of_row[:, None] >= jnp.arange(count)[None, :]
    q_heads = queries.reshape(count, local_heads, group * HD)
    q_rows = q_heads[:, 0].reshape(count * group, HD)
    near_keys = fresh[:, 0:HD]
    near_vals = fresh[:, HD : 2 * HD]
    near_scores = rows_by_keys(q_rows, near_keys) * scale
    top = jnp.max(jnp.where(near_mask, near_scores, -1e30), axis=1)
    weights = jnp.where(near_mask, jnp.exp(near_scores - top[:, None]), 0.0)
    total = jnp.sum(weights, axis=1)
    numer = jnp.dot(weights.astype(jnp.bfloat16), near_vals, preferred_element_type=jnp.float32)

    def visit(carry, block_rows):
        keys = block_rows[:, 0:HD]
        vals = block_rows[:, HD : 2 * HD]
        scores = rows_by_keys(q_rows, keys) * scale
        return (merge(carry, scores, mask, vals), None)

    (top, total, numer), unused = lax.scan(visit, (top, total, numer), grouped)
    results = (numer / total[:, None]).reshape(count, group * HD)
    attended = results.astype(jnp.bfloat16)
    return (attended, fresh)


def solution(mesh):
    npool = mesh.shape["pool"]
    ntp = mesh.shape["tp"]
    nx = 4 if npool % 8 == 0 else 1
    nz = npool // (2 * nx)
    nzh = 4 if nz % 4 == 0 else 1
    fine = Mesh(
        np.asarray(mesh.devices).reshape(nx, nzh, nz // nzh, 2, ntp),
        ("px", "pzh", "pzl", "pc", "tp"),
    )
    placed = (
        P(POOL, "tp"),
        P("tp", POOL),
        P(POOL, "tp"),
        P(POOL, None, "tp"),
        P(POOL, None),
        P(POOL, None, None),
    )
    return jax.shard_map(
        body,
        mesh=fine,
        in_specs=placed,
        out_specs=(P(POOL, "tp"), P(POOL, "tp")),
        check_vma=False,
    )
```

```python
import math

import jax
import jax.numpy as jnp
import numpy as np
from jax import lax
from jax.sharding import Mesh
from jax.sharding import PartitionSpec as P

HD = 128
QH = 32
KVH = 4
BLK = 128
RBLK = 64
POOL = ("px", "pz", "pc")
ID_SPLIT = 32


def rows_by_keys(left, right):
    return lax.dot_general(
        left, right, (((1,), (1,)), ((), ())), preferred_element_type=jnp.float32
    )


def merge(carry, scores, mask, vals):
    top_now, total_now, numer_now = carry
    top_new = jnp.maximum(top_now, jnp.max(jnp.where(mask, scores, -1e30), axis=1))
    weights_now = jnp.where(mask, jnp.exp(scores - top_new[:, None]), 0.0)
    factor = jnp.exp(top_now - top_new)
    total_new = total_now * factor + jnp.sum(weights_now, axis=1)
    numer_new = numer_now * factor[:, None] + jnp.dot(
        weights_now.astype(jnp.bfloat16), vals, preferred_element_type=jnp.float32
    )
    return (top_new, total_new, numer_new)


def body(hidden_rows, kv_weight, queries, cache_table, retrieval, pattern):
    blocks_dev, blk, width = cache_table.shape
    npool = lax.axis_size(POOL)
    fetch_count = retrieval.shape[1]
    wanted = retrieval[0]
    id_row = jnp.concatenate(
        [
            (wanted // ID_SPLIT).astype(jnp.bfloat16),
            (wanted % ID_SPLIT).astype(jnp.bfloat16),
            jnp.zeros((width - 2 * fetch_count,), jnp.bfloat16),
        ]
    )
    id_block = jnp.broadcast_to(id_row[None, None, :], (1, blk, width))
    outgoing = jnp.concatenate([cache_table, id_block], axis=0)
    nx, nz, nc = (lax.axis_size(a) for a in POOL)
    rows_out = blocks_dev + 1
    step = outgoing.reshape(rows_out, nx, nz, nc, width).transpose(0, 1, 3, 2, 4)
    step = step.reshape(rows_out, nx * nc, nz, width)
    step = lax.all_to_all(step, ("px", "pc"), split_axis=1, concat_axis=1, tiled=True)
    step = lax.all_to_all(step, "pz", split_axis=2, concat_axis=2, tiled=True)
    step = step.reshape(rows_out, nx, nc, nz, width).transpose(1, 3, 2, 0, 4)
    by_token = step.reshape(npool, rows_out, width)
    table = by_token[:, :blocks_dev].reshape(npool * blocks_dev, width)
    id_rows = by_token[:, blocks_dev].astype(jnp.float32)
    wanted_all = (
        id_rows[:, :fetch_count] * ID_SPLIT + id_rows[:, fetch_count : 2 * fetch_count]
    ).astype(jnp.int32)
    picks = (
        wanted_all.reshape(-1)[:, None]
        == jnp.arange(npool * blocks_dev, dtype=jnp.int32)[None, :]
    ).astype(jnp.bfloat16)
    reply = jnp.dot(picks, table, preferred_element_type=jnp.bfloat16)
    reply = reply.reshape(npool, fetch_count, 1, width)
    reply, hidden_rows, kv_weight = lax.optimization_barrier((reply, hidden_rows, kv_weight))
    fetched = lax.all_to_all(reply, POOL, split_axis=0, concat_axis=0, tiled=True)

    w_head = lax.all_gather(kv_weight, ("pz", "pc"), axis=1, tiled=True)
    w_all = lax.all_gather(w_head, "px", axis=1, tiled=True)
    partial_kv = jnp.dot(hidden_rows, w_all, preferred_element_type=jnp.float32)
    fresh = lax.psum_scatter(partial_kv.astype(jnp.bfloat16), "tp", scatter_dimension=1, tiled=True)

    count = hidden_rows.shape[0]
    group = QH // KVH
    scale = float(HD) ** (-0.5)
    local_heads = fresh.shape[1] // (2 * HD)
    tokens_step = BLK // math.gcd(BLK, 8)
    steps_count = BLK // tokens_step
    grouped = fetched.reshape(steps_count, tokens_step * fetch_count, width)
    token_of_row = jnp.arange(count * group) // group
    block_of_row = token_of_row // RBLK
    row_pat = jnp.take(pattern[0] != 0, block_of_row, axis=0)
    mask = jnp.tile(row_pat, (1, tokens_step))
    near_mask = token_of_row[:, None] >= jnp.arange(count)[None, :]
    q_heads = queries.reshape(count, local_heads, group * HD)
    q_rows = q_heads[:, 0].reshape(count * group, HD)
    near_keys = fresh[:, 0:HD]
    near_vals = fresh[:, HD : 2 * HD]
    near_scores = rows_by_keys(q_rows, near_keys) * scale
    top = jnp.max(jnp.where(near_mask, near_scores, -1e30), axis=1)
    weights = jnp.where(near_mask, jnp.exp(near_scores - top[:, None]), 0.0)
    total = jnp.sum(weights, axis=1)
    numer = jnp.dot(weights.astype(jnp.bfloat16), near_vals, preferred_element_type=jnp.float32)

    def visit(carry, block_rows):
        keys = block_rows[:, 0:HD]
        vals = block_rows[:, HD : 2 * HD]
        scores = rows_by_keys(q_rows, keys) * scale
        return (merge(carry, scores, mask, vals), None)

    (top, total, numer), unused = lax.scan(visit, (top, total, numer), grouped)
    results = (numer / total[:, None]).reshape(count, group * HD)
    attended = results.astype(jnp.bfloat16)
    return (attended, fresh)


def solution(mesh):
    npool = mesh.shape["pool"]
    ntp = mesh.shape["tp"]
    nx = 4 if npool % 8 == 0 else 1
    fine = Mesh(
        np.asarray(mesh.devices).reshape(nx, npool // (2 * nx), 2, ntp),
        ("px", "pz", "pc", "tp"),
    )
    placed = (
        P(POOL, "tp"),
        P("tp", POOL),
        P(POOL, "tp"),
        P(POOL, None, "tp"),
        P(POOL, None),
        P(POOL, None, None),
    )
    return jax.shard_map(
        body,
        mesh=fine,
        in_specs=placed,
        out_specs=(P(POOL, "tp"), P(POOL, "tp")),
        check_vma=False,
    )
```

```python
import math

import jax
import jax.numpy as jnp
import numpy as np
from jax import lax
from jax.sharding import Mesh
from jax.sharding import PartitionSpec as P

HD = 128
QH = 32
KVH = 4
BLK = 128
RBLK = 64
POOL = ("px", "pz", "pc")
ID_SPLIT = 32


def rows_by_keys(left, right):
    return lax.dot_general(
        left, right, (((1,), (1,)), ((), ())), preferred_element_type=jnp.float32
    )


def merge(carry, scores, mask, vals):
    top_now, total_now, numer_now = carry
    top_new = jnp.maximum(top_now, jnp.max(jnp.where(mask, scores, -1e30), axis=1))
    weights_now = jnp.where(mask, jnp.exp(scores - top_new[:, None]), 0.0)
    factor = jnp.exp(top_now - top_new)
    total_new = total_now * factor + jnp.sum(weights_now, axis=1)
    numer_new = numer_now * factor[:, None] + jnp.dot(
        weights_now.astype(jnp.bfloat16), vals, preferred_element_type=jnp.float32
    )
    return (top_new, total_new, numer_new)


def body(hidden_rows, kv_weight, queries, cache_table, retrieval, pattern):
    blocks_dev, blk, width = cache_table.shape
    npool = lax.axis_size(POOL)
    fetch_count = retrieval.shape[1]
    wanted = retrieval[0]
    id_row = jnp.concatenate(
        [
            (wanted // ID_SPLIT).astype(jnp.bfloat16),
            (wanted % ID_SPLIT).astype(jnp.bfloat16),
            jnp.zeros((width - 2 * fetch_count,), jnp.bfloat16),
        ]
    )
    id_block = jnp.broadcast_to(id_row[None, None, :], (1, blk, width))
    outgoing = jnp.concatenate([cache_table, id_block], axis=0)
    nx, nz, nc = (lax.axis_size(a) for a in POOL)
    rows_out = blocks_dev + 1
    step = outgoing.reshape(rows_out, nx, nz, nc, width).transpose(0, 1, 3, 2, 4)
    step = step.reshape(rows_out, nx * nc, nz, width)
    step = lax.all_to_all(step, ("px", "pc"), split_axis=1, concat_axis=1, tiled=True)
    step = lax.all_to_all(step, "pz", split_axis=2, concat_axis=2, tiled=True)
    step = step.reshape(rows_out, nx, nc, nz, width).transpose(1, 3, 2, 0, 4)
    by_token = step.reshape(npool, rows_out, width)
    table = by_token[:, :blocks_dev].reshape(npool * blocks_dev, width)
    id_rows = by_token[:, blocks_dev].astype(jnp.float32)
    wanted_all = (
        id_rows[:, :fetch_count] * ID_SPLIT + id_rows[:, fetch_count : 2 * fetch_count]
    ).astype(jnp.int32)
    picks = (
        wanted_all.reshape(-1)[:, None]
        == jnp.arange(npool * blocks_dev, dtype=jnp.int32)[None, :]
    ).astype(jnp.bfloat16)
    reply = jnp.dot(picks, table, preferred_element_type=jnp.float32).astype(jnp.bfloat16)
    reply = reply.reshape(npool, fetch_count, 1, width)
    reply, hidden_rows, kv_weight = lax.optimization_barrier((reply, hidden_rows, kv_weight))
    fetched = lax.all_to_all(reply, POOL, split_axis=0, concat_axis=0, tiled=True)

    w_head = lax.all_gather(kv_weight, ("pz", "pc"), axis=1, tiled=True)
    w_all = lax.all_gather(w_head, "px", axis=1, tiled=True)
    partial_kv = jnp.dot(hidden_rows, w_all, preferred_element_type=jnp.float32)
    fresh = lax.psum_scatter(partial_kv.astype(jnp.bfloat16), "tp", scatter_dimension=1, tiled=True)

    count = hidden_rows.shape[0]
    group = QH // KVH
    scale = float(HD) ** (-0.5)
    local_heads = fresh.shape[1] // (2 * HD)
    tokens_step = BLK // math.gcd(BLK, 4)
    steps_count = BLK // tokens_step
    grouped = fetched.reshape(steps_count, tokens_step * fetch_count, width)
    token_of_row = jnp.arange(count * group) // group
    block_of_row = token_of_row // RBLK
    row_pat = jnp.take(pattern[0] != 0, block_of_row, axis=0)
    mask = jnp.tile(row_pat, (1, tokens_step))
    near_mask = token_of_row[:, None] >= jnp.arange(count)[None, :]
    q_heads = queries.reshape(count, local_heads, group * HD)
    q_rows = q_heads[:, 0].reshape(count * group, HD)
    near_keys = fresh[:, 0:HD]
    near_vals = fresh[:, HD : 2 * HD]
    near_scores = rows_by_keys(q_rows, near_keys) * scale
    top = jnp.max(jnp.where(near_mask, near_scores, -1e30), axis=1)
    weights = jnp.where(near_mask, jnp.exp(near_scores - top[:, None]), 0.0)
    total = jnp.sum(weights, axis=1)
    numer = jnp.dot(weights.astype(jnp.bfloat16), near_vals, preferred_element_type=jnp.float32)

    def visit(carry, block_rows):
        keys = block_rows[:, 0:HD]
        vals = block_rows[:, HD : 2 * HD]
        scores = rows_by_keys(q_rows, keys) * scale
        return (merge(carry, scores, mask, vals), None)

    (top, total, numer), unused = lax.scan(visit, (top, total, numer), grouped)
    results = (numer / total[:, None]).reshape(count, group * HD)
    attended = results.astype(jnp.bfloat16)
    return (attended, fresh)


def solution(mesh):
    npool = mesh.shape["pool"]
    ntp = mesh.shape["tp"]
    nx = 4 if npool % 8 == 0 else 1
    fine = Mesh(
        np.asarray(mesh.devices).reshape(nx, npool // (2 * nx), 2, ntp),
        ("px", "pz", "pc", "tp"),
    )
    placed = (
        P(POOL, "tp"),
        P("tp", POOL),
        P(POOL, "tp"),
        P(POOL, None, "tp"),
        P(POOL, None),
        P(POOL, None, None),
    )
    return jax.shard_map(
        body,
        mesh=fine,
        in_specs=placed,
        out_specs=(P(POOL, "tp"), P(POOL, "tp")),
        check_vma=False,
    )
```
